256 devices in a mesh: seq: 32 (over z, x), dp: 8 (over y, core).
Axes of the slice: x: 4, y: 4, z: 8, core: 2. Of those that a mesh axis runs over, the one named last changes fastest.
Arguments:
- query_rows: bfloat16 [8, 4096, 2048], P('dp', 'seq'), may hold values from -6 to 6
- key_rows: bfloat16 [8, 4096, 2048], P('dp', 'seq'), may hold values from -6 to 6
- value_rows: bfloat16 [8, 4096, 2048], P('dp', 'seq'), may hold values from -6 to 6
- out_grad: bfloat16 [8, 4096, 4096], P('dp', 'seq'), may hold values from -6 to 6
- rand_blocks: int32 [8, 64, 3], P('dp'), may hold values from 0 to 63
- global_tokens: int32 [8, 128], P('dp'), may hold values from 0 to 4095, as said below
- out_proj: bfloat16 [2048, 4096], P('dp'), may hold values from -0.125 to 0.125
Outputs:
- grad_queries: bfloat16 [8, 4096, 2048], P('dp', 'seq')
- grad_keys: bfloat16 [8, 4096, 2048], P('dp', 'seq')
- grad_values: bfloat16 [8, 4096, 2048], P('dp', 'seq')
- grad_out_proj: bfloat16 [2048, 4096], P('dp')
The draws below stay inside these ranges and needn't reach their ends.
Inputs may be any that keep to these rules, and one draw needn't show every extreme that they name: `global_tokens`: in each document window 128 distinct positions in increasing order; the first and the last position of the window are always among them.
All inputs are finite; a program needn't handle non-finite values.
Results may differ from the reference program's by a relative error of at most 0.012.
Values may be sent and summed in bfloat16 or wider, within the bound.
No kernel may reach another device: no remote copies, remote signals or barrier semaphores. Data moves between devices by JAX's collectives and lax.ppermute only.
A program may use at most 128 MiB of HBM per device.

```python
import math
import jax
import jax.numpy as jnp
from jax import lax

D = 4096
HEADS = 16
HEAD_DIM = 128
BLOCK = 64
RANDOM = 3
GLOBALS = 128
DOCS = 8
SEQ = 4096
NBLOCKS = 64


def drawn_pair(seed_key):
    shape = (DOCS, SEQ, HEADS * HEAD_DIM)
    query_out = jax.random.normal(jax.random.fold_in(seed_key, 21), shape, jnp.float32)
    key_out = jax.random.normal(jax.random.fold_in(seed_key, 22), shape, jnp.float32)
    return (jnp.clip(query_out, -6.0, 6.0), jnp.clip(key_out, -6.0, 6.0))


def draw_query_rows(key, part):
    return drawn_pair(key)[0].astype(jnp.bfloat16)


def draw_key_rows(key, part):
    return drawn_pair(key)[1].astype(jnp.bfloat16)


def one_global_set(doc_key):
    inner = jax.random.permutation(doc_key, SEQ - 2)[:GLOBALS - 2] + 1
    chosen = jnp.concatenate([jnp.array([0, SEQ - 1], dtype=jnp.int32), inner.astype(jnp.int32)])
    return jnp.sort(chosen).astype(jnp.int32)


def draw_global_tokens(key, part):
    doc_keys = jax.random.split(jax.random.fold_in(key, 31), DOCS)
    return jax.vmap(one_global_set)(doc_keys)


def place_ends(result, rng, least, largest):
    place = [jax.random.randint(jax.random.fold_in(rng, axis), (), 0, length) for axis, length in enumerate(result.shape)]
    longest = result.shape.index(max(result.shape))
    beside = place[:longest] + [(place[longest] + 1) % result.shape[longest]] + place[longest + 1:]
    return result.at[tuple(place)].set(least).at[tuple(beside)].set(largest)


def steps_of(stream_key, shape, pieces, low, high):
    def one(dim, shards_of):
        steps = jax.random.uniform(jax.random.fold_in(jax.random.fold_in(stream_key, 6), dim), (shards_of,), jnp.float32, low / len(pieces), high / len(pieces))
        return jnp.repeat(jnp.exp(steps), shape[dim] // shards_of).reshape((-1,) + (1,) * (len(shape) - dim - 1))

    loudness = one(*pieces[0])
    for cut in pieces[1:]:
        loudness = loudness * one(*cut)
    return loudness


def normal_values(own_key, extent, scale, limit, cuts=(), kind=jnp.bfloat16):
    values = jax.random.normal(own_key, extent, jnp.float32) * scale
    if len(cuts) > 0:
        values = steps_of(own_key, extent, cuts, -0.22, 0.18) * values
    return jnp.clip(values, min=-limit, max=limit).astype(kind)


def setup_inputs(seed: int = 0) -> dict:
    streams_of = jax.random.split(jax.random.key(seed), 8)
    return {
        "query_rows": draw_query_rows(jax.random.fold_in(streams_of[7], 71), 0),
        "key_rows": draw_key_rows(jax.random.fold_in(streams_of[7], 71), 0),
        "value_rows": normal_values(streams_of[2], (DOCS, SEQ, HEADS * HEAD_DIM), 1.0, 6.0, ((0, 8), (1, 32))),
        "out_grad": normal_values(streams_of[3], (DOCS, SEQ, D), 1.0, 6.0, ((0, 8), (1, 32))),
        "rand_blocks": place_ends(jax.random.randint(streams_of[4], (DOCS, NBLOCKS, RANDOM), 0, NBLOCKS), jax.random.fold_in(streams_of[4], 1), 0, NBLOCKS - 1).astype(jnp.int32),
        "global_tokens": draw_global_tokens(jax.random.fold_in(streams_of[7], 71), 0),
        "out_proj": normal_values(streams_of[6], (HEADS * HEAD_DIM, D), (HEADS * HEAD_DIM) ** -0.5, 0.125, ((0, 8),)),
    }


MASKED = -1e+30

def softmax_rows(scores):
    highest = lax.optimization_barrier(jnp.max(scores, axis=-1, keepdims=True))
    raised = jnp.exp(scores - highest)
    return raised / lax.optimization_barrier(jnp.sum(raised, axis=-1, keepdims=True))

def rounded(numbers):
    return lax.optimization_barrier(numbers.astype(jnp.bfloat16)).astype(jnp.float32)

def block_lists(doc_blocks):
    blocks = jnp.arange(NBLOCKS, dtype=jnp.int32)
    window = blocks[:, None] + jnp.arange(-1, 2, dtype=jnp.int32)[None, :]
    inside = (window >= 0) & (window < NBLOCKS)
    block_ids = jnp.concatenate([jnp.clip(window, 0, NBLOCKS - 1), doc_blocks.astype(jnp.int32)], axis=1)
    usable = jnp.concatenate([jnp.repeat(inside, BLOCK, axis=1), jnp.ones((NBLOCKS, RANDOM * BLOCK), dtype=bool)], axis=1)
    return (block_ids, usable)

def reference(query_rows, key_rows, value_rows, out_grad, rand_blocks, global_tokens, out_proj):
    width = HEADS * HEAD_DIM
    window_keys = (3 + RANDOM) * BLOCK
    scaling = 1.0 / math.sqrt(HEAD_DIM)

    def one_document(totals, document):
        query_doc, key_doc, value_doc, grad_doc, doc_blocks, doc_globals = document
        block_ids, usable = block_lists(doc_blocks)
        positions = jnp.arange(SEQ, dtype=jnp.int32)
        is_global = jnp.any(positions[:, None] == doc_globals[None, :], axis=1)
        keep_rows = jnp.where(is_global, 0.0, 1.0).astype(jnp.float32).reshape(NBLOCKS, 1, BLOCK, 1)
        query_all = query_doc.astype(jnp.float32).reshape(SEQ, HEADS, HEAD_DIM)
        key_all = key_doc.astype(jnp.float32).reshape(SEQ, HEADS, HEAD_DIM)
        value_all = value_doc.astype(jnp.float32).reshape(SEQ, HEADS, HEAD_DIM)
        query_blk = query_all.reshape(NBLOCKS, BLOCK, HEADS, HEAD_DIM)
        key_win = key_all.reshape(NBLOCKS, BLOCK, HEADS, HEAD_DIM)[block_ids].reshape(NBLOCKS, window_keys, HEADS, HEAD_DIM)
        value_win = value_all.reshape(NBLOCKS, BLOCK, HEADS, HEAD_DIM)[block_ids].reshape(NBLOCKS, window_keys, HEADS, HEAD_DIM)
        key_glob = key_all[doc_globals]
        value_glob = value_all[doc_globals]
        score_win = jnp.einsum('bqhe,bkhe->bhqk', query_blk, key_win) * scaling
        score_win = jnp.where(usable[:, None, None, :], score_win, MASKED)
        score_glob = jnp.einsum('bqhe,khe->bhqk', query_blk, key_glob) * scaling
        prob_rows = softmax_rows(jnp.concatenate([score_win, score_glob], axis=-1))
        prob_bf = rounded(prob_rows)
        sparse_out = jnp.einsum('bhqk,bkhe->bqhe', prob_bf[..., :window_keys], value_win)
        sparse_out = sparse_out + jnp.einsum('bhqk,khe->bqhe', prob_bf[..., window_keys:], value_glob)
        query_glob = query_all[doc_globals]
        prob_glob = softmax_rows(jnp.einsum('ghe,the->hgt', query_glob, key_all) * scaling)
        prob_glob_bf = rounded(prob_glob)
        glob_out = jnp.einsum('hgt,the->ghe', prob_glob_bf, value_all).reshape(GLOBALS, width)
        attention = sparse_out.reshape(SEQ, width).at[doc_globals].set(glob_out).astype(jnp.bfloat16)
        out_delta = jnp.dot(grad_doc, out_proj.T, preferred_element_type=jnp.float32).astype(jnp.bfloat16)
        totals = totals + jnp.dot(attention.T, grad_doc, preferred_element_type=jnp.float32)
        delta_all = out_delta.astype(jnp.float32).reshape(SEQ, HEADS, HEAD_DIM)
        delta_blk = delta_all.reshape(NBLOCKS, BLOCK, HEADS, HEAD_DIM)
        prob_grad = jnp.concatenate([jnp.einsum('bqhe,bkhe->bhqk', delta_blk, value_win), jnp.einsum('bqhe,khe->bhqk', delta_blk, value_glob)], axis=-1)
        score_grad = prob_rows * (prob_grad - lax.optimization_barrier(jnp.sum(prob_rows * prob_grad, axis=-1, keepdims=True))) * keep_rows
        score_bf = rounded(score_grad)
        prob_kept = prob_bf * keep_rows
        grad_query = jnp.einsum('bhqk,bkhe->bqhe', score_bf[..., :window_keys], key_win)
        grad_query = (grad_query + jnp.einsum('bhqk,khe->bqhe', score_bf[..., window_keys:], key_glob)).reshape(SEQ, width) * scaling
        flat_ids = block_ids.reshape(-1)
        key_part = jnp.einsum('bhqk,bqhe->bkhe', score_bf[..., :window_keys], query_blk).reshape(NBLOCKS * (3 + RANDOM), BLOCK, width) * scaling
        grad_key = jnp.zeros((NBLOCKS, BLOCK, width), jnp.float32).at[flat_ids].add(key_part).reshape(SEQ, width)
        key_globpart = jnp.einsum('bhqk,bqhe->khe', score_bf[..., window_keys:], query_blk).reshape(GLOBALS, width) * scaling
        grad_key = grad_key.at[doc_globals].add(key_globpart)
        value_part = jnp.einsum('bhqk,bqhe->bkhe', prob_kept[..., :window_keys], delta_blk).reshape(NBLOCKS * (3 + RANDOM), BLOCK, width)
        grad_value = jnp.zeros((NBLOCKS, BLOCK, width), jnp.float32).at[flat_ids].add(value_part).reshape(SEQ, width)
        value_globpart = jnp.einsum('bhqk,bqhe->khe', prob_kept[..., window_keys:], delta_blk).reshape(GLOBALS, width)
        grad_value = grad_value.at[doc_globals].add(value_globpart)
        delta_glob = delta_all[doc_globals]
        prob_grad_glob = jnp.einsum('ghe,the->hgt', delta_glob, value_all)
        score_glob_bf = rounded(prob_glob * (prob_grad_glob - lax.optimization_barrier(jnp.sum(prob_glob * prob_grad_glob, axis=-1, keepdims=True))))
        grad_query = grad_query.at[doc_globals].add(jnp.einsum('hgt,the->ghe', score_glob_bf, key_all).reshape(GLOBALS, width) * scaling)
        grad_key = grad_key + jnp.einsum('hgt,ghe->the', score_glob_bf, query_glob).reshape(SEQ, width) * scaling
        grad_value = grad_value + jnp.einsum('hgt,ghe->the', prob_glob_bf, delta_glob).reshape(SEQ, width)
        return (totals, (grad_query.astype(jnp.bfloat16), grad_key.astype(jnp.bfloat16), grad_value.astype(jnp.bfloat16)))
    totals, (grad_queries, grad_keys, grad_values) = lax.scan(one_document, jnp.zeros((width, D), jnp.float32), (query_rows, key_rows, value_rows, out_grad, rand_blocks, global_tokens))
    return (grad_queries, grad_keys, grad_values, totals.astype(jnp.bfloat16))
```

```python
import math

import jax
import jax.numpy as jnp
from jax import lax
from jax.sharding import PartitionSpec as P

HEAD_DIM = 128
BLOCK = 64
RANDOM = 3


MASKED = -1e30


def softmax_rows(scores):
    highest = jnp.max(scores, axis=-1, keepdims=True)
    raised = jnp.exp(scores - highest)
    return raised / jnp.sum(raised, axis=-1, keepdims=True)


def shards(query_rows, key_rows, value_rows, out_grad, rand_blocks, global_tokens, out_proj):
    seq_devices = lax.axis_size("seq")
    dp_devices = lax.axis_size("dp")
    tokens = query_rows.shape[1]
    width = query_rows.shape[2]
    model_width = out_grad.shape[2]
    head_count = width // HEAD_DIM
    splitting = max(seq_devices // head_count, 1)
    heads_here = max(head_count // seq_devices, 1)
    columns = heads_here * HEAD_DIM
    head_groups = seq_devices // splitting
    slice_rows = tokens // splitting
    seq_length = tokens * seq_devices
    block_total = seq_length // BLOCK
    window_keys = (3 + RANDOM) * BLOCK
    query_count = seq_devices * slice_rows
    query_blocks = query_count // BLOCK
    owned_groups = seq_devices // dp_devices // splitting
    global_count = global_tokens.shape[1]
    scaling = 1.0 / math.sqrt(HEAD_DIM)
    my_slice = lax.axis_index("seq") % splitting
    doc_blocks = rand_blocks[0]
    doc_globals = global_tokens[0]
    query_send = (
        query_rows[0]
        .reshape(splitting, slice_rows, head_groups, columns)
        .transpose(2, 0, 1, 3)
        .reshape(seq_devices, slice_rows, columns)
    )

    def spread(rows):
        grouped = rows[0].reshape(tokens, head_groups, columns).transpose(1, 0, 2)
        return jnp.broadcast_to(
            grouped[:, None], (head_groups, splitting, tokens, columns)
        ).reshape(seq_devices, tokens, columns)

    query_head, key_head, value_head = (
        lax.all_to_all(query_send, "seq", split_axis=0, concat_axis=0, tiled=True),
        lax.all_to_all(spread(key_rows), "seq", split_axis=0, concat_axis=0, tiled=True),
        lax.all_to_all(spread(value_rows), "seq", split_axis=0, concat_axis=0, tiled=True),
    )
    source_start = jnp.arange(seq_devices, dtype=jnp.int32)[:, None] * tokens
    offsets = jnp.arange(slice_rows, dtype=jnp.int32)[None, :]
    query_pos = (source_start + my_slice * slice_rows + offsets).reshape(query_count)
    block_of = query_pos.reshape(query_blocks, BLOCK)[:, 0] // BLOCK
    window = block_of[:, None] + jnp.arange(-1, 2, dtype=jnp.int32)[None, :]
    inside = (window >= 0) & (window < block_total)
    block_ids = jnp.concatenate(
        [jnp.clip(window, 0, block_total - 1), jnp.take(doc_blocks, block_of, axis=0)], axis=1
    )
    usable = jnp.concatenate(
        [jnp.repeat(inside, BLOCK, axis=1), jnp.ones((query_blocks, RANDOM * BLOCK), dtype=bool)],
        axis=1,
    )
    key_all = key_head.reshape(seq_length, heads_here, HEAD_DIM)
    value_all = value_head.reshape(seq_length, heads_here, HEAD_DIM)
    key_win = key_all.reshape(block_total, BLOCK, heads_here, HEAD_DIM)[block_ids].reshape(
        query_blocks, window_keys, heads_here, HEAD_DIM
    )
    value_win = value_all.reshape(block_total, BLOCK, heads_here, HEAD_DIM)[block_ids].reshape(
        query_blocks, window_keys, heads_here, HEAD_DIM
    )
    key_glob = jnp.take(key_all, doc_globals, axis=0)
    value_glob = jnp.take(value_all, doc_globals, axis=0)
    query_blk = query_head.reshape(query_blocks, BLOCK, heads_here, HEAD_DIM)
    score_win = (
        jnp.einsum("bqhe,bkhe->bhqk", query_blk, key_win, preferred_element_type=jnp.float32)
        * scaling
    )
    score_win = jnp.where(usable[:, None, None, :], score_win, MASKED)
    score_glob = (
        jnp.einsum("bqhe,khe->bhqk", query_blk, key_glob, preferred_element_type=jnp.float32)
        * scaling
    )
    prob_rows = softmax_rows(jnp.concatenate([score_win, score_glob], axis=-1))
    prob_bf = prob_rows.astype(jnp.bfloat16)
    sparse_out = jnp.einsum(
        "bhqk,bkhe->bqhe", prob_bf[..., :window_keys], value_win, preferred_element_type=jnp.float32
    )
    sparse_out = sparse_out + jnp.einsum(
        "bhqk,khe->bqhe", prob_bf[..., window_keys:], value_glob, preferred_element_type=jnp.float32
    )
    matches = query_pos[:, None] == doc_globals[None, :]
    picker = matches.astype(jnp.bfloat16)
    picker_f = matches.astype(jnp.float32)
    is_global = jnp.any(matches, axis=1)
    query_glob = (
        jnp.einsum(
            "ng,nc->gc",
            picker,
            query_head.reshape(query_count, columns),
            preferred_element_type=jnp.float32,
        )
        .astype(jnp.bfloat16)
        .reshape(global_count, heads_here, HEAD_DIM)
    )
    prob_glob = softmax_rows(
        jnp.einsum("ghe,the->hgt", query_glob, key_all, preferred_element_type=jnp.float32)
        * scaling
    )
    prob_glob_bf = prob_glob.astype(jnp.bfloat16)
    glob_out = jnp.einsum(
        "hgt,the->ghe", prob_glob_bf, value_all, preferred_element_type=jnp.float32
    ).reshape(global_count, columns)
    placed = jnp.dot(picker_f, glob_out, precision=lax.Precision.HIGHEST)
    attention = jnp.where(
        is_global[:, None], placed, sparse_out.reshape(query_count, columns)
    ).astype(jnp.bfloat16)
    owned = lax.all_to_all(
        lax.all_to_all(
            attention.reshape(1, seq_devices, slice_rows, columns),
            "seq",
            split_axis=1,
            concat_axis=1,
            tiled=True,
        ),
        "dp",
        split_axis=1,
        concat_axis=0,
        tiled=True,
    )
    owned = owned.reshape(dp_devices, owned_groups, splitting, slice_rows, columns)
    proj_rows = out_proj.reshape(owned_groups, columns, model_width)
    piece_rows = lax.all_gather(out_grad, "dp", axis=0, tiled=True)
    doc_count = piece_rows.shape[0]
    grads = piece_rows.reshape(doc_count, splitting, slice_rows, model_width)
    local_delta = jnp.einsum(
        "kptd,gcd->kgptc", grads, proj_rows, preferred_element_type=jnp.float32
    ).astype(jnp.bfloat16)
    local_delta = local_delta.reshape(doc_count, owned_groups * splitting, slice_rows, columns)
    delta_blocks = local_delta
    grad_sum = jnp.einsum("kgptc,kptd->gcd", owned, grads, preferred_element_type=jnp.float32)
    grad_sum, delta_blocks = (grad_sum, delta_blocks)
    grad_part = lax.psum_scatter(
        grad_sum.reshape(width // dp_devices, model_width), "seq", scatter_dimension=0, tiled=True
    )
    grad_out_proj = lax.all_gather(grad_part.astype(jnp.bfloat16), "seq", axis=0, tiled=True)
    delta_head = lax.all_to_all(
        lax.all_to_all(delta_blocks, "dp", split_axis=0, concat_axis=1, tiled=True),
        "seq",
        split_axis=1,
        concat_axis=1,
        tiled=True,
    )
    delta_blk = delta_head.reshape(query_blocks, BLOCK, heads_here, HEAD_DIM)
    prob_grad = jnp.concatenate(
        [
            jnp.einsum("bqhe,bkhe->bhqk", delta_blk, value_win, preferred_element_type=jnp.float32),
            jnp.einsum("bqhe,khe->bhqk", delta_blk, value_glob, preferred_element_type=jnp.float32),
        ],
        axis=-1,
    )
    keep_rows = (
        jnp.where(is_global, 0.0, 1.0).astype(jnp.float32).reshape(query_blocks, 1, BLOCK, 1)
    )
    score_bf = (
        prob_rows * (prob_grad - jnp.sum(prob_rows * prob_grad, axis=-1, keepdims=True)) * keep_rows
    ).astype(jnp.bfloat16)
    prob_kept = prob_bf * keep_rows.astype(jnp.bfloat16)
    grad_query = jnp.einsum(
        "bhqk,bkhe->bqhe", score_bf[..., :window_keys], key_win, preferred_element_type=jnp.float32
    )
    grad_query = (
        grad_query
        + jnp.einsum(
            "bhqk,khe->bqhe",
            score_bf[..., window_keys:],
            key_glob,
            preferred_element_type=jnp.float32,
        )
    ) * scaling
    flat_ids = block_ids.reshape(-1)
    key_part = (
        jnp.einsum(
            "bhqk,bqhe->bkhe",
            score_bf[..., :window_keys],
            query_blk,
            preferred_element_type=jnp.float32,
        )
        * scaling
    )
    key_globpart = (
        jnp.einsum(
            "bhqk,bqhe->khe",
            score_bf[..., window_keys:],
            query_blk,
            preferred_element_type=jnp.float32,
        )
        * scaling
    )
    value_part = jnp.einsum(
        "bhqk,bqhe->bkhe",
        prob_kept[..., :window_keys],
        delta_blk,
        preferred_element_type=jnp.float32,
    )
    value_globpart = jnp.einsum(
        "bhqk,bqhe->khe",
        prob_kept[..., window_keys:],
        delta_blk,
        preferred_element_type=jnp.float32,
    )
    grad_key = (
        jnp.zeros((block_total, BLOCK, columns), jnp.float32)
        .at[flat_ids]
        .add(key_part.reshape(-1, BLOCK, columns))
        .reshape(seq_length, columns)
    )
    grad_key = grad_key.at[doc_globals].add(key_globpart.reshape(global_count, columns))
    grad_value = (
        jnp.zeros((block_total, BLOCK, columns), jnp.float32)
        .at[flat_ids]
        .add(value_part.reshape(-1, BLOCK, columns))
        .reshape(seq_length, columns)
    )
    grad_value = grad_value.at[doc_globals].add(value_globpart.reshape(global_count, columns))
    delta_glob = (
        jnp.einsum(
            "ng,nc->gc",
            picker,
            delta_head.reshape(query_count, columns),
            preferred_element_type=jnp.float32,
        )
        .astype(jnp.bfloat16)
        .reshape(global_count, heads_here, HEAD_DIM)
    )
    prob_grad_glob = jnp.einsum(
        "ghe,the->hgt", delta_glob, value_all, preferred_element_type=jnp.float32
    )
    score_glob_bf = (
        prob_glob * (prob_grad_glob - jnp.sum(prob_glob * prob_grad_glob, axis=-1, keepdims=True))
    ).astype(jnp.bfloat16)
    grad_query_glob = (
        jnp.einsum(
            "hgt,the->ghe", score_glob_bf, key_all, preferred_element_type=jnp.float32
        ).reshape(global_count, columns)
        * scaling
    )
    grad_key = (
        grad_key
        + jnp.einsum(
            "hgt,ghe->the", score_glob_bf, query_glob, preferred_element_type=jnp.float32
        ).reshape(seq_length, columns)
        * scaling
    )
    grad_value = grad_value + jnp.einsum(
        "hgt,ghe->the", prob_glob_bf, delta_glob, preferred_element_type=jnp.float32
    ).reshape(seq_length, columns)
    grad_query_all = grad_query.reshape(query_count, columns) + jnp.dot(
        picker_f, grad_query_glob, precision=lax.Precision.HIGHEST
    )
    query_back, key_back, value_back = (
        lax.all_to_all(
            grad_query_all.astype(jnp.bfloat16).reshape(seq_devices, slice_rows, columns),
            "seq",
            split_axis=0,
            concat_axis=0,
            tiled=True,
        ),
        lax.all_to_all(
            grad_key.astype(jnp.bfloat16).reshape(seq_devices, tokens, columns),
            "seq",
            split_axis=0,
            concat_axis=0,
            tiled=True,
        ),
        lax.all_to_all(
            grad_value.astype(jnp.bfloat16).reshape(seq_devices, tokens, columns),
            "seq",
            split_axis=0,
            concat_axis=0,
            tiled=True,
        ),
    )

    def fold_pairs(received):
        summed = jnp.sum(
            received.astype(jnp.float32).reshape(head_groups, splitting, tokens, columns), axis=1
        )
        return summed.transpose(1, 0, 2).reshape(1, tokens, width).astype(jnp.bfloat16)

    grad_queries = (
        query_back.reshape(head_groups, splitting, slice_rows, columns)
        .transpose(1, 2, 0, 3)
        .reshape(1, tokens, width)
        .astype(jnp.bfloat16)
    )
    grad_keys = fold_pairs(key_back)
    grad_values = fold_pairs(value_back)
    return (grad_queries, grad_keys, grad_values, grad_out_proj)


def solution(mesh):
    return jax.shard_map(
        shards,
        mesh=mesh,
        in_specs=(
            P("dp", "seq", None),
            P("dp", "seq", None),
            P("dp", "seq", None),
            P("dp", "seq", None),
            P("dp", None, None),
            P("dp", None),
            P("dp", None),
        ),
        out_specs=(P("dp", "seq", None), P("dp", "seq", None), P("dp", "seq", None), P("dp", None)),
        check_vma=False,
    )
```

```python
import math

import jax
import jax.numpy as jnp
from jax import lax
from jax.sharding import Mesh, PartitionSpec as P

HEAD_DIM = 128
BLOCK = 64
RANDOM = 3


MASKED = -1e30
SEQ_AXES = ("sz", "sx")
DP_AXES = ("dy", "dc")


def softmax_rows(scores):
    highest = jnp.max(scores, axis=-1, keepdims=True)
    raised = jnp.exp(scores - highest)
    return raised / jnp.sum(raised, axis=-1, keepdims=True)


def shards(query_rows, key_rows, value_rows, out_grad, rand_blocks, global_tokens, out_proj):
    seq_devices = lax.axis_size(SEQ_AXES)
    dp_devices = lax.axis_size(DP_AXES)
    tokens = query_rows.shape[1]
    width = query_rows.shape[2]
    model_width = out_grad.shape[2]
    head_count = width // HEAD_DIM
    splitting = max(seq_devices // head_count, 1)
    heads_here = max(head_count // seq_devices, 1)
    columns = heads_here * HEAD_DIM
    head_groups = seq_devices // splitting
    slice_rows = tokens // splitting
    seq_length = tokens * seq_devices
    block_total = seq_length // BLOCK
    window_keys = (3 + RANDOM) * BLOCK
    query_count = seq_devices * slice_rows
    query_blocks = query_count // BLOCK
    owned_groups = seq_devices // dp_devices // splitting
    global_count = global_tokens.shape[1]
    scaling = 1.0 / math.sqrt(HEAD_DIM)
    my_slice = lax.axis_index(SEQ_AXES) % splitting
    doc_blocks = rand_blocks[0]
    doc_globals = global_tokens[0]
    query_send = (
        query_rows[0]
        .reshape(splitting, slice_rows, head_groups, columns)
        .transpose(2, 0, 1, 3)
        .reshape(seq_devices, slice_rows, columns)
    )

    def spread(rows):
        grouped = rows[0].reshape(tokens, head_groups, columns).transpose(1, 0, 2)
        return jnp.broadcast_to(
            grouped[:, None], (head_groups, splitting, tokens, columns)
        ).reshape(seq_devices, tokens, columns)

    query_head, key_head, value_head = (
        lax.all_to_all(query_send, SEQ_AXES, split_axis=0, concat_axis=0, tiled=True),
        lax.all_to_all(spread(key_rows), SEQ_AXES, split_axis=0, concat_axis=0, tiled=True),
        lax.all_to_all(spread(value_rows), SEQ_AXES, split_axis=0, concat_axis=0, tiled=True),
    )
    source_start = jnp.arange(seq_devices, dtype=jnp.int32)[:, None] * tokens
    offsets = jnp.arange(slice_rows, dtype=jnp.int32)[None, :]
    query_pos = (source_start + my_slice * slice_rows + offsets).reshape(query_count)
    block_of = query_pos.reshape(query_blocks, BLOCK)[:, 0] // BLOCK
    window = block_of[:, None] + jnp.arange(-1, 2, dtype=jnp.int32)[None, :]
    inside = (window >= 0) & (window < block_total)
    block_ids = jnp.concatenate(
        [jnp.clip(window, 0, block_total - 1), jnp.take(doc_blocks, block_of, axis=0)], axis=1
    )
    usable = jnp.concatenate(
        [jnp.repeat(inside, BLOCK, axis=1), jnp.ones((query_blocks, RANDOM * BLOCK), dtype=bool)],
        axis=1,
    )
    key_all = key_head.reshape(seq_length, heads_here, HEAD_DIM)
    value_all = value_head.reshape(seq_length, heads_here, HEAD_DIM)
    key_win = key_all.reshape(block_total, BLOCK, heads_here, HEAD_DIM)[block_ids].reshape(
        query_blocks, window_keys, heads_here, HEAD_DIM
    )
    value_win = value_all.reshape(block_total, BLOCK, heads_here, HEAD_DIM)[block_ids].reshape(
        query_blocks, window_keys, heads_here, HEAD_DIM
    )
    key_glob = jnp.take(key_all, doc_globals, axis=0)
    value_glob = jnp.take(value_all, doc_globals, axis=0)
    query_blk = query_head.reshape(query_blocks, BLOCK, heads_here, HEAD_DIM)
    score_win = (
        jnp.einsum("bqhe,bkhe->bhqk", query_blk, key_win, preferred_element_type=jnp.float32)
        * scaling
    )
    score_win = jnp.where(usable[:, None, None, :], score_win, MASKED)
    score_glob = (
        jnp.einsum("bqhe,khe->bhqk", query_blk, key_glob, preferred_element_type=jnp.float32)
        * scaling
    )
    prob_rows = softmax_rows(jnp.concatenate([score_win, score_glob], axis=-1))
    prob_bf = prob_rows.astype(jnp.bfloat16)
    sparse_out = jnp.einsum(
        "bhqk,bkhe->bqhe", prob_bf[..., :window_keys], value_win, preferred_element_type=jnp.float32
    )
    sparse_out = sparse_out + jnp.einsum(
        "bhqk,khe->bqhe", prob_bf[..., window_keys:], value_glob, preferred_element_type=jnp.float32
    )
    matches = query_pos[:, None] == doc_globals[None, :]
    picker = matches.astype(jnp.bfloat16)
    picker_f = matches.astype(jnp.float32)
    is_global = jnp.any(matches, axis=1)
    query_glob = (
        jnp.einsum(
            "ng,nc->gc",
            picker,
            query_head.reshape(query_count, columns),
            preferred_element_type=jnp.float32,
        )
        .astype(jnp.bfloat16)
        .reshape(global_count, heads_here, HEAD_DIM)
    )
    prob_glob = softmax_rows(
        jnp.einsum("ghe,the->hgt", query_glob, key_all, preferred_element_type=jnp.float32)
        * scaling
    )
    prob_glob_bf = prob_glob.astype(jnp.bfloat16)
    glob_out = jnp.einsum(
        "hgt,the->ghe", prob_glob_bf, value_all, preferred_element_type=jnp.float32
    ).reshape(global_count, columns)
    placed = jnp.dot(picker_f, glob_out, precision=lax.Precision.HIGHEST)
    attention = jnp.where(
        is_global[:, None], placed, sparse_out.reshape(query_count, columns)
    ).astype(jnp.bfloat16)
    owned = lax.all_to_all(
        lax.all_to_all(
            attention.reshape(1, seq_devices, slice_rows, columns),
            SEQ_AXES,
            split_axis=1,
            concat_axis=1,
            tiled=True,
        ),
        DP_AXES,
        split_axis=1,
        concat_axis=0,
        tiled=True,
    )
    owned = owned.reshape(dp_devices, owned_groups, splitting, slice_rows, columns)
    proj_rows = out_proj.reshape(owned_groups, columns, model_width)
    piece_rows = lax.all_gather(out_grad, DP_AXES, axis=0, tiled=True)
    doc_count = piece_rows.shape[0]
    grads = piece_rows.reshape(doc_count, splitting, slice_rows, model_width)
    local_delta = jnp.einsum(
        "kptd,gcd->kgptc", grads, proj_rows, preferred_element_type=jnp.float32
    ).astype(jnp.bfloat16)
    local_delta = local_delta.reshape(doc_count, owned_groups * splitting, slice_rows, columns)
    delta_blocks = local_delta
    grad_sum = jnp.einsum("kgptc,kptd->gcd", owned, grads, preferred_element_type=jnp.float32)
    grad_sum, delta_blocks = (grad_sum, delta_blocks)
    z_size = lax.axis_size("sz")
    x_size = lax.axis_size("sx")
    proj_part = grad_sum.reshape(width // dp_devices, model_width).astype(jnp.bfloat16)
    x_rows = proj_part.shape[0] // x_size
    x_sum = jnp.sum(
        lax.all_to_all(
            proj_part.reshape(x_size, x_rows, model_width), "sx", 0, 0, tiled=True
        ).astype(jnp.float32),
        axis=0,
    )
    z_rows = x_rows // z_size
    z_sum = jnp.sum(
        lax.all_to_all(
            x_sum.astype(jnp.bfloat16).reshape(z_size, z_rows, model_width), "sz", 0, 0, tiled=True
        ).astype(jnp.float32),
        axis=0,
    )
    grad_out_proj = lax.all_gather(
        lax.all_gather(z_sum.astype(jnp.bfloat16), "sz", axis=0, tiled=True), "sx", axis=0, tiled=True
    )
    delta_head = lax.all_to_all(
        lax.all_to_all(delta_blocks, DP_AXES, split_axis=0, concat_axis=1, tiled=True),
        SEQ_AXES,
        split_axis=1,
        concat_axis=1,
        tiled=True,
    )
    delta_blk = delta_head.reshape(query_blocks, BLOCK, heads_here, HEAD_DIM)
    prob_grad = jnp.concatenate(
        [
            jnp.einsum("bqhe,bkhe->bhqk", delta_blk, value_win, preferred_element_type=jnp.float32),
            jnp.einsum("bqhe,khe->bhqk", delta_blk, value_glob, preferred_element_type=jnp.float32),
        ],
        axis=-1,
    )
    keep_rows = (
        jnp.where(is_global, 0.0, 1.0).astype(jnp.float32).reshape(query_blocks, 1, BLOCK, 1)
    )
    score_bf = (
        prob_rows * (prob_grad - jnp.sum(prob_rows * prob_grad, axis=-1, keepdims=True)) * keep_rows
    ).astype(jnp.bfloat16)
    prob_kept = prob_bf * keep_rows.astype(jnp.bfloat16)
    grad_query = jnp.einsum(
        "bhqk,bkhe->bqhe", score_bf[..., :window_keys], key_win, preferred_element_type=jnp.float32
    )
    grad_query = (
        grad_query
        + jnp.einsum(
            "bhqk,khe->bqhe",
            score_bf[..., window_keys:],
            key_glob,
            preferred_element_type=jnp.float32,
        )
    ) * scaling
    flat_ids = block_ids.reshape(-1)
    key_part = (
        jnp.einsum(
            "bhqk,bqhe->bkhe",
            score_bf[..., :window_keys],
            query_blk,
            preferred_element_type=jnp.float32,
        )
        * scaling
    )
    key_globpart = (
        jnp.einsum(
            "bhqk,bqhe->khe",
            score_bf[..., window_keys:],
            query_blk,
            preferred_element_type=jnp.float32,
        )
        * scaling
    )
    value_part = jnp.einsum(
        "bhqk,bqhe->bkhe",
        prob_kept[..., :window_keys],
        delta_blk,
        preferred_element_type=jnp.float32,
    )
    value_globpart = jnp.einsum(
        "bhqk,bqhe->khe",
        prob_kept[..., window_keys:],
        delta_blk,
        preferred_element_type=jnp.float32,
    )
    block_hot = (flat_ids[:, None] == jnp.arange(block_total, dtype=jnp.int32)[None, :]).astype(
        jnp.float32
    )

    def place_blocks(parts):
        return jnp.einsum(
            "nb,nx->bx",
            block_hot,
            parts.reshape(block_hot.shape[0], BLOCK * columns),
            precision=lax.Precision.HIGHEST,
            preferred_element_type=jnp.float32,
        ).reshape(seq_length, columns)

    grad_key = place_blocks(key_part)
    grad_key = grad_key.at[doc_globals].add(key_globpart.reshape(global_count, columns))
    grad_value = place_blocks(value_part)
    grad_value = grad_value.at[doc_globals].add(value_globpart.reshape(global_count, columns))
    delta_glob = (
        jnp.einsum(
            "ng,nc->gc",
            picker,
            delta_head.reshape(query_count, columns),
            preferred_element_type=jnp.float32,
        )
        .astype(jnp.bfloat16)
        .reshape(global_count, heads_here, HEAD_DIM)
    )
    prob_grad_glob = jnp.einsum(
        "ghe,the->hgt", delta_glob, value_all, preferred_element_type=jnp.float32
    )
    score_glob_bf = (
        prob_glob * (prob_grad_glob - jnp.sum(prob_glob * prob_grad_glob, axis=-1, keepdims=True))
    ).astype(jnp.bfloat16)
    grad_query_glob = (
        jnp.einsum(
            "hgt,the->ghe", score_glob_bf, key_all, preferred_element_type=jnp.float32
        ).reshape(global_count, columns)
        * scaling
    )
    grad_key = (
        grad_key
        + jnp.einsum(
            "hgt,ghe->the", score_glob_bf, query_glob, preferred_element_type=jnp.float32
        ).reshape(seq_length, columns)
        * scaling
    )
    grad_value = grad_value + jnp.einsum(
        "hgt,ghe->the", prob_glob_bf, delta_glob, preferred_element_type=jnp.float32
    ).reshape(seq_length, columns)
    grad_query_all = grad_query.reshape(query_count, columns) + jnp.dot(
        picker_f, grad_query_glob, precision=lax.Precision.HIGHEST
    )
    query_back, key_back, value_back = (
        lax.all_to_all(
            grad_query_all.astype(jnp.bfloat16).reshape(seq_devices, slice_rows, columns),
            SEQ_AXES,
            split_axis=0,
            concat_axis=0,
            tiled=True,
        ),
        lax.all_to_all(
            grad_key.astype(jnp.bfloat16).reshape(seq_devices, tokens, columns),
            SEQ_AXES,
            split_axis=0,
            concat_axis=0,
            tiled=True,
        ),
        lax.all_to_all(
            grad_value.astype(jnp.bfloat16).reshape(seq_devices, tokens, columns),
            SEQ_AXES,
            split_axis=0,
            concat_axis=0,
            tiled=True,
        ),
    )

    def fold_pairs(received):
        summed = jnp.sum(
            received.astype(jnp.float32).reshape(head_groups, splitting, tokens, columns), axis=1
        )
        return summed.transpose(1, 0, 2).reshape(1, tokens, width).astype(jnp.bfloat16)

    grad_queries = (
        query_back.reshape(head_groups, splitting, slice_rows, columns)
        .transpose(1, 2, 0, 3)
        .reshape(1, tokens, width)
        .astype(jnp.bfloat16)
    )
    grad_keys = fold_pairs(key_back)
    grad_values = fold_pairs(value_back)
    return (grad_queries, grad_keys, grad_values, grad_out_proj)


def solution(mesh):
    seq_size, dp_size = mesh.shape["seq"], mesh.shape["dp"]
    torus = Mesh(
        mesh.devices.reshape(seq_size // 4, 4, dp_size // 2, 2), SEQ_AXES + DP_AXES
    )
    return jax.shard_map(
        shards,
        mesh=torus,
        in_specs=(
            P(DP_AXES, SEQ_AXES, None),
            P(DP_AXES, SEQ_AXES, None),
            P(DP_AXES, SEQ_AXES, None),
            P(DP_AXES, SEQ_AXES, None),
            P(DP_AXES, None, None),
            P(DP_AXES, None),
            P(DP_AXES, None),
        ),
        out_specs=(P(DP_AXES, SEQ_AXES, None), P(DP_AXES, SEQ_AXES, None), P(DP_AXES, SEQ_AXES, None), P(DP_AXES, None)),
        check_vma=False,
    )
```

```python
import math

import jax
import jax.numpy as jnp
from jax import lax
from jax.sharding import Mesh, PartitionSpec as P

HEAD_DIM = 128
BLOCK = 64
RANDOM = 3


MASKED = -1e30
SEQ_AXES = ("sz", "sx")
DP_AXES = ("dy", "dc")


def softmax_rows(scores):
    highest = jnp.max(scores, axis=-1, keepdims=True)
    raised = jnp.exp(scores - highest)
    return raised / jnp.sum(raised, axis=-1, keepdims=True)


def shards(query_rows, key_rows, value_rows, out_grad, rand_blocks, global_tokens, out_proj):
    seq_devices = lax.axis_size(SEQ_AXES)
    dp_devices = lax.axis_size(DP_AXES)
    tokens = query_rows.shape[1]
    width = query_rows.shape[2]
    model_width = out_grad.shape[2]
    head_count = width // HEAD_DIM
    splitting = max(seq_devices // head_count, 1)
    heads_here = max(head_count // seq_devices, 1)
    columns = heads_here * HEAD_DIM
    head_groups = seq_devices // splitting
    slice_rows = tokens // splitting
    seq_length = tokens * seq_devices
    block_total = seq_length // BLOCK
    window_keys = (3 + RANDOM) * BLOCK
    query_count = seq_devices * slice_rows
    query_blocks = query_count // BLOCK
    owned_groups = seq_devices // dp_devices // splitting
    global_count = global_tokens.shape[1]
    scaling = 1.0 / math.sqrt(HEAD_DIM)
    my_slice = lax.axis_index(SEQ_AXES) % splitting
    doc_blocks = rand_blocks[0]
    doc_globals = global_tokens[0]
    query_send = (
        query_rows[0]
        .reshape(splitting, slice_rows, head_groups, columns)
        .transpose(2, 0, 1, 3)
        .reshape(seq_devices, slice_rows, columns)
    )

    def spread(rows):
        grouped = rows[0].reshape(tokens, head_groups, columns).transpose(1, 0, 2)
        return jnp.broadcast_to(
            grouped[:, None], (head_groups, splitting, tokens, columns)
        ).reshape(seq_devices, tokens, columns)

    query_head, key_head, value_head = (
        lax.all_to_all(query_send, SEQ_AXES, split_axis=0, concat_axis=0, tiled=True),
        lax.all_to_all(spread(key_rows), SEQ_AXES, split_axis=0, concat_axis=0, tiled=True),
        lax.all_to_all(spread(value_rows), SEQ_AXES, split_axis=0, concat_axis=0, tiled=True),
    )
    source_start = jnp.arange(seq_devices, dtype=jnp.int32)[:, None] * tokens
    offsets = jnp.arange(slice_rows, dtype=jnp.int32)[None, :]
    query_pos = (source_start + my_slice * slice_rows + offsets).reshape(query_count)
    block_of = query_pos.reshape(query_blocks, BLOCK)[:, 0] // BLOCK
    window = block_of[:, None] + jnp.arange(-1, 2, dtype=jnp.int32)[None, :]
    inside = (window >= 0) & (window < block_total)
    block_ids = jnp.concatenate(
        [jnp.clip(window, 0, block_total - 1), jnp.take(doc_blocks, block_of, axis=0)], axis=1
    )
    usable = jnp.concatenate(
        [jnp.repeat(inside, BLOCK, axis=1), jnp.ones((query_blocks, RANDOM * BLOCK), dtype=bool)],
        axis=1,
    )
    key_all = key_head.reshape(seq_length, heads_here, HEAD_DIM)
    value_all = value_head.reshape(seq_length, heads_here, HEAD_DIM)
    key_win = key_all.reshape(block_total, BLOCK, heads_here, HEAD_DIM)[block_ids].reshape(
        query_blocks, window_keys, heads_here, HEAD_DIM
    )
    value_win = value_all.reshape(block_total, BLOCK, heads_here, HEAD_DIM)[block_ids].reshape(
        query_blocks, window_keys, heads_here, HEAD_DIM
    )
    key_glob = jnp.take(key_all, doc_globals, axis=0)
    value_glob = jnp.take(value_all, doc_globals, axis=0)
    query_blk = query_head.reshape(query_blocks, BLOCK, heads_here, HEAD_DIM)
    score_win = (
        jnp.einsum("bqhe,bkhe->bhqk", query_blk, key_win, preferred_element_type=jnp.float32)
        * scaling
    )
    score_win = jnp.where(usable[:, None, None, :], score_win, MASKED)
    score_glob = (
        jnp.einsum("bqhe,khe->bhqk", query_blk, key_glob, preferred_element_type=jnp.float32)
        * scaling
    )
    prob_rows = softmax_rows(jnp.concatenate([score_win, score_glob], axis=-1))
    prob_bf = prob_rows.astype(jnp.bfloat16)
    sparse_out = jnp.einsum(
        "bhqk,bkhe->bqhe", prob_bf[..., :window_keys], value_win, preferred_element_type=jnp.float32
    )
    sparse_out = sparse_out + jnp.einsum(
        "bhqk,khe->bqhe", prob_bf[..., window_keys:], value_glob, preferred_element_type=jnp.float32
    )
    matches = query_pos[:, None] == doc_globals[None, :]
    picker = matches.astype(jnp.bfloat16)
    picker_f = matches.astype(jnp.float32)
    is_global = jnp.any(matches, axis=1)
    query_glob = (
        jnp.einsum(
            "ng,nc->gc",
            picker,
            query_head.reshape(query_count, columns),
            preferred_element_type=jnp.float32,
        )
        .astype(jnp.bfloat16)
        .reshape(global_count, heads_here, HEAD_DIM)
    )
    prob_glob = softmax_rows(
        jnp.einsum("ghe,the->hgt", query_glob, key_all, preferred_element_type=jnp.float32)
        * scaling
    )
    prob_glob_bf = prob_glob.astype(jnp.bfloat16)
    glob_out = jnp.einsum(
        "hgt,the->ghe", prob_glob_bf, value_all, preferred_element_type=jnp.float32
    ).reshape(global_count, columns)
    placed = jnp.dot(picker_f, glob_out, precision=lax.Precision.HIGHEST)
    attention = jnp.where(
        is_global[:, None], placed, sparse_out.reshape(query_count, columns)
    ).astype(jnp.bfloat16)
    owned = lax.all_to_all(
        lax.all_to_all(
            attention.reshape(1, seq_devices, slice_rows, columns),
            SEQ_AXES,
            split_axis=1,
            concat_axis=1,
            tiled=True,
        ),
        DP_AXES,
        split_axis=1,
        concat_axis=0,
        tiled=True,
    )
    owned = owned.reshape(dp_devices, owned_groups, splitting, slice_rows, columns)
    proj_rows = out_proj.reshape(owned_groups, columns, model_width)
    piece_rows = lax.all_gather(out_grad, DP_AXES, axis=0, tiled=True)
    doc_count = piece_rows.shape[0]
    grads = piece_rows.reshape(doc_count, splitting, slice_rows, model_width)
    local_delta = jnp.einsum(
        "kptd,gcd->kgptc", grads, proj_rows, preferred_element_type=jnp.float32
    ).astype(jnp.bfloat16)
    local_delta = local_delta.reshape(doc_count, owned_groups * splitting, slice_rows, columns)
    delta_blocks = local_delta
    grad_sum = jnp.einsum("kgptc,kptd->gcd", owned, grads, preferred_element_type=jnp.float32)
    grad_sum, delta_blocks = (grad_sum, delta_blocks)
    z_size = lax.axis_size("sz")
    x_size = lax.axis_size("sx")
    proj_part = grad_sum.reshape(width // dp_devices, model_width).astype(jnp.bfloat16)
    z_rows = proj_part.shape[0] // (x_size * z_size)
    x_sum = jnp.sum(
        lax.all_to_all(
            proj_part.reshape(z_size, x_size, z_rows, model_width).transpose(1, 0, 2, 3),
            "sx",
            0,
            0,
            tiled=True,
        ).astype(jnp.float32),
        axis=0,
    )
    z_sum = jnp.sum(
        lax.all_to_all(
            x_sum.astype(jnp.bfloat16).reshape(z_size, z_rows, model_width), "sz", 0, 0, tiled=True
        ).astype(jnp.float32),
        axis=0,
    )
    grad_out_proj = lax.all_gather(z_sum.astype(jnp.bfloat16), SEQ_AXES, axis=0, tiled=True)
    delta_head = lax.all_to_all(
        lax.all_to_all(delta_blocks, DP_AXES, split_axis=0, concat_axis=1, tiled=True),
        SEQ_AXES,
        split_axis=1,
        concat_axis=1,
        tiled=True,
    )
    delta_blk = delta_head.reshape(query_blocks, BLOCK, heads_here, HEAD_DIM)
    prob_grad = jnp.concatenate(
        [
            jnp.einsum("bqhe,bkhe->bhqk", delta_blk, value_win, preferred_element_type=jnp.float32),
            jnp.einsum("bqhe,khe->bhqk", delta_blk, value_glob, preferred_element_type=jnp.float32),
        ],
        axis=-1,
    )
    keep_rows = (
        jnp.where(is_global, 0.0, 1.0).astype(jnp.float32).reshape(query_blocks, 1, BLOCK, 1)
    )
    score_bf = (
        prob_rows * (prob_grad - jnp.sum(prob_rows * prob_grad, axis=-1, keepdims=True)) * keep_rows
    ).astype(jnp.bfloat16)
    prob_kept = prob_bf * keep_rows.astype(jnp.bfloat16)
    grad_query = jnp.einsum(
        "bhqk,bkhe->bqhe", score_bf[..., :window_keys], key_win, preferred_element_type=jnp.float32
    )
    grad_query = (
        grad_query
        + jnp.einsum(
            "bhqk,khe->bqhe",
            score_bf[..., window_keys:],
            key_glob,
            preferred_element_type=jnp.float32,
        )
    ) * scaling
    flat_ids = block_ids.reshape(-1)
    key_part = (
        jnp.einsum(
            "bhqk,bqhe->bkhe",
            score_bf[..., :window_keys],
            query_blk,
            preferred_element_type=jnp.float32,
        )
        * scaling
    )
    key_globpart = (
        jnp.einsum(
            "bhqk,bqhe->khe",
            score_bf[..., window_keys:],
            query_blk,
            preferred_element_type=jnp.float32,
        )
        * scaling
    )
    value_part = jnp.einsum(
        "bhqk,bqhe->bkhe",
        prob_kept[..., :window_keys],
        delta_blk,
        preferred_element_type=jnp.float32,
    )
    value_globpart = jnp.einsum(
        "bhqk,bqhe->khe",
        prob_kept[..., window_keys:],
        delta_blk,
        preferred_element_type=jnp.float32,
    )
    block_hot = (block_ids[:, :, None] == jnp.arange(block_total, dtype=jnp.int32)).astype(
        jnp.float32
    )

    def place_blocks(parts):
        return jnp.einsum(
            "bjc,bjke->cke",
            block_hot,
            parts.reshape(query_blocks, 3 + RANDOM, BLOCK, columns),
            precision=lax.Precision.HIGHEST,
            preferred_element_type=jnp.float32,
        ).reshape(seq_length, columns)

    grad_key = place_blocks(key_part)
    grad_key = grad_key.at[doc_globals].add(key_globpart.reshape(global_count, columns))
    grad_value = place_blocks(value_part)
    grad_value = grad_value.at[doc_globals].add(value_globpart.reshape(global_count, columns))
    delta_glob = (
        jnp.einsum(
            "ng,nc->gc",
            picker,
            delta_head.reshape(query_count, columns),
            preferred_element_type=jnp.float32,
        )
        .astype(jnp.bfloat16)
        .reshape(global_count, heads_here, HEAD_DIM)
    )
    prob_grad_glob = jnp.einsum(
        "ghe,the->hgt", delta_glob, value_all, preferred_element_type=jnp.float32
    )
    score_glob_bf = (
        prob_glob * (prob_grad_glob - jnp.sum(prob_glob * prob_grad_glob, axis=-1, keepdims=True))
    ).astype(jnp.bfloat16)
    grad_query_glob = (
        jnp.einsum(
            "hgt,the->ghe", score_glob_bf, key_all, preferred_element_type=jnp.float32
        ).reshape(global_count, columns)
        * scaling
    )
    grad_key = (
        grad_key
        + jnp.einsum(
            "hgt,ghe->the", score_glob_bf, query_glob, preferred_element_type=jnp.float32
        ).reshape(seq_length, columns)
        * scaling
    )
    grad_value = grad_value + jnp.einsum(
        "hgt,ghe->the", prob_glob_bf, delta_glob, preferred_element_type=jnp.float32
    ).reshape(seq_length, columns)
    grad_query_all = grad_query.reshape(query_count, columns) + jnp.dot(
        picker_f, grad_query_glob, precision=lax.Precision.HIGHEST
    )
    query_back, key_back, value_back = (
        lax.all_to_all(
            grad_query_all.astype(jnp.bfloat16).reshape(seq_devices, slice_rows, columns),
            SEQ_AXES,
            split_axis=0,
            concat_axis=0,
            tiled=True,
        ),
        lax.all_to_all(
            grad_key.astype(jnp.bfloat16).reshape(seq_devices, tokens, columns),
            SEQ_AXES,
            split_axis=0,
            concat_axis=0,
            tiled=True,
        ),
        lax.all_to_all(
            grad_value.astype(jnp.bfloat16).reshape(seq_devices, tokens, columns),
            SEQ_AXES,
            split_axis=0,
            concat_axis=0,
            tiled=True,
        ),
    )

    def fold_pairs(received):
        summed = jnp.sum(
            received.astype(jnp.float32).reshape(head_groups, splitting, tokens, columns), axis=1
        )
        return summed.transpose(1, 0, 2).reshape(1, tokens, width).astype(jnp.bfloat16)

    grad_queries = (
        query_back.reshape(head_groups, splitting, slice_rows, columns)
        .transpose(1, 2, 0, 3)
        .reshape(1, tokens, width)
        .astype(jnp.bfloat16)
    )
    grad_keys = fold_pairs(key_back)
    grad_values = fold_pairs(value_back)
    return (grad_queries, grad_keys, grad_values, grad_out_proj)


def solution(mesh):
    seq_size, dp_size = mesh.shape["seq"], mesh.shape["dp"]
    torus = Mesh(
        mesh.devices.reshape(seq_size // 4, 4, dp_size // 2, 2), SEQ_AXES + DP_AXES
    )
    return jax.shard_map(
        shards,
        mesh=torus,
        in_specs=(
            P(DP_AXES, SEQ_AXES, None),
            P(DP_AXES, SEQ_AXES, None),
            P(DP_AXES, SEQ_AXES, None),
            P(DP_AXES, SEQ_AXES, None),
            P(DP_AXES, None, None),
            P(DP_AXES, None),
            P(DP_AXES, None),
        ),
        out_specs=(P(DP_AXES, SEQ_AXES, None), P(DP_AXES, SEQ_AXES, None), P(DP_AXES, SEQ_AXES, None), P(DP_AXES, None)),
        check_vma=False,
    )
```

```python
import math

import jax
import jax.numpy as jnp
from jax import lax
from jax.sharding import Mesh, PartitionSpec as P

HEAD_DIM = 128
BLOCK = 64
RANDOM = 3


MASKED = -1e30
SEQ_AXES = ("sz", "sx")
DP_AXES = ("dy", "dc")


def softmax_rows(scores):
    highest = jnp.max(scores, axis=-1, keepdims=True)
    raised = jnp.exp(scores - highest)
    return raised / jnp.sum(raised, axis=-1, keepdims=True)


def shards(query_rows, key_rows, value_rows, out_grad, rand_blocks, global_tokens, out_proj):
    seq_devices = lax.axis_size(SEQ_AXES)
    dp_devices = lax.axis_size(DP_AXES)
    tokens = query_rows.shape[1]
    width = query_rows.shape[2]
    model_width = out_grad.shape[2]
    head_count = width // HEAD_DIM
    splitting = max(seq_devices // head_count, 1)
    heads_here = max(head_count // seq_devices, 1)
    columns = heads_here * HEAD_DIM
    head_groups = seq_devices // splitting
    slice_rows = tokens // splitting
    seq_length = tokens * seq_devices
    block_total = seq_length // BLOCK
    window_keys = (3 + RANDOM) * BLOCK
    query_count = seq_devices * slice_rows
    query_blocks = query_count // BLOCK
    owned_groups = seq_devices // dp_devices // splitting
    global_count = global_tokens.shape[1]
    scaling = 1.0 / math.sqrt(HEAD_DIM)
    my_slice = lax.axis_index(SEQ_AXES) % splitting
    doc_blocks = rand_blocks[0]
    doc_globals = global_tokens[0]
    def head_rows(rows):
        return (
            rows[0]
            .reshape(splitting, slice_rows, head_groups, columns)
            .transpose(2, 0, 1, 3)
            .reshape(seq_devices, slice_rows, columns)
        )

    partner = [(i, i ^ 1) for i in range(lax.axis_size("sx"))]

    def both_halves(mine):
        other = lax.ppermute(mine, "sx", partner)
        low = jnp.where(my_slice == 0, mine, other)
        high = jnp.where(my_slice == 0, other, mine)
        return jnp.stack([low, high], axis=1).reshape(seq_devices, tokens, columns)

    def to_heads(rows):
        return lax.all_to_all(head_rows(rows), SEQ_AXES, split_axis=0, concat_axis=0, tiled=True)

    query_head = to_heads(query_rows)
    key_head = both_halves(to_heads(key_rows))
    value_head = both_halves(to_heads(value_rows))
    source_start = jnp.arange(seq_devices, dtype=jnp.int32)[:, None] * tokens
    offsets = jnp.arange(slice_rows, dtype=jnp.int32)[None, :]
    query_pos = (source_start + my_slice * slice_rows + offsets).reshape(query_count)
    block_of = query_pos.reshape(query_blocks, BLOCK)[:, 0] // BLOCK
    window = block_of[:, None] + jnp.arange(-1, 2, dtype=jnp.int32)[None, :]
    inside = (window >= 0) & (window < block_total)
    block_ids = jnp.concatenate(
        [jnp.clip(window, 0, block_total - 1), jnp.take(doc_blocks, block_of, axis=0)], axis=1
    )
    usable = jnp.concatenate(
        [jnp.repeat(inside, BLOCK, axis=1), jnp.ones((query_blocks, RANDOM * BLOCK), dtype=bool)],
        axis=1,
    )
    key_all = key_head.reshape(seq_length, heads_here, HEAD_DIM)
    value_all = value_head.reshape(seq_length, heads_here, HEAD_DIM)
    key_win = key_all.reshape(block_total, BLOCK, heads_here, HEAD_DIM)[block_ids].reshape(
        query_blocks, window_keys, heads_here, HEAD_DIM
    )
    value_win = value_all.reshape(block_total, BLOCK, heads_here, HEAD_DIM)[block_ids].reshape(
        query_blocks, window_keys, heads_here, HEAD_DIM
    )
    key_glob = jnp.take(key_all, doc_globals, axis=0)
    value_glob = jnp.take(value_all, doc_globals, axis=0)
    query_blk = query_head.reshape(query_blocks, BLOCK, heads_here, HEAD_DIM)
    score_win = (
        jnp.einsum("bqhe,bkhe->bhqk", query_blk, key_win, preferred_element_type=jnp.float32)
        * scaling
    )
    score_win = jnp.where(usable[:, None, None, :], score_win, MASKED)
    score_glob = (
        jnp.einsum("bqhe,khe->bhqk", query_blk, key_glob, preferred_element_type=jnp.float32)
        * scaling
    )
    prob_rows = softmax_rows(jnp.concatenate([score_win, score_glob], axis=-1))
    prob_bf = prob_rows.astype(jnp.bfloat16)
    sparse_out = jnp.einsum(
        "bhqk,bkhe->bqhe", prob_bf[..., :window_keys], value_win, preferred_element_type=jnp.float32
    )
    sparse_out = sparse_out + jnp.einsum(
        "bhqk,khe->bqhe", prob_bf[..., window_keys:], value_glob, preferred_element_type=jnp.float32
    )
    matches = query_pos[:, None] == doc_globals[None, :]
    picker = matches.astype(jnp.bfloat16)
    picker_f = matches.astype(jnp.float32)
    is_global = jnp.any(matches, axis=1)
    query_glob = (
        jnp.einsum(
            "ng,nc->gc",
            picker,
            query_head.reshape(query_count, columns),
            preferred_element_type=jnp.float32,
        )
        .astype(jnp.bfloat16)
        .reshape(global_count, heads_here, HEAD_DIM)
    )
    prob_glob = softmax_rows(
        jnp.einsum("ghe,the->hgt", query_glob, key_all, preferred_element_type=jnp.float32)
        * scaling
    )
    prob_glob_bf = prob_glob.astype(jnp.bfloat16)
    glob_out = jnp.einsum(
        "hgt,the->ghe", prob_glob_bf, value_all, preferred_element_type=jnp.float32
    ).reshape(global_count, columns)
    placed = jnp.dot(picker_f, glob_out, precision=lax.Precision.HIGHEST)
    attention = jnp.where(
        is_global[:, None], placed, sparse_out.reshape(query_count, columns)
    ).astype(jnp.bfloat16)
    owned = lax.all_to_all(
        lax.all_to_all(
            attention.reshape(1, seq_devices, slice_rows, columns),
            SEQ_AXES,
            split_axis=1,
            concat_axis=1,
            tiled=True,
        ),
        DP_AXES,
        split_axis=1,
        concat_axis=0,
        tiled=True,
    )
    owned = owned.reshape(dp_devices, owned_groups, splitting, slice_rows, columns)
    proj_rows = out_proj.reshape(owned_groups, columns, model_width)
    piece_rows = lax.all_gather(out_grad, DP_AXES, axis=0, tiled=True)
    doc_count = piece_rows.shape[0]
    grads = piece_rows.reshape(doc_count, splitting, slice_rows, model_width)
    local_delta = jnp.einsum(
        "kptd,gcd->kgptc", grads, proj_rows, preferred_element_type=jnp.float32
    ).astype(jnp.bfloat16)
    local_delta = local_delta.reshape(doc_count, owned_groups * splitting, slice_rows, columns)
    delta_blocks = local_delta
    grad_sum = jnp.einsum("kgptc,kptd->gcd", owned, grads, preferred_element_type=jnp.float32)
    grad_sum, delta_blocks = (grad_sum, delta_blocks)
    z_size = lax.axis_size("sz")
    x_size = lax.axis_size("sx")
    proj_part = grad_sum.reshape(width // dp_devices, model_width).astype(jnp.bfloat16)
    z_rows = proj_part.shape[0] // (x_size * z_size)
    x_sum = jnp.sum(
        lax.all_to_all(
            proj_part.reshape(z_size, x_size, z_rows, model_width).transpose(1, 0, 2, 3),
            "sx",
            0,
            0,
            tiled=True,
        ).astype(jnp.float32),
        axis=0,
    )
    z_sum = jnp.sum(
        lax.all_to_all(
            x_sum.astype(jnp.bfloat16).reshape(z_size, z_rows, model_width), "sz", 0, 0, tiled=True
        ).astype(jnp.float32),
        axis=0,
    )
    grad_out_proj = lax.all_gather(z_sum.astype(jnp.bfloat16), SEQ_AXES, axis=0, tiled=True)
    delta_head = lax.all_to_all(
        lax.all_to_all(delta_blocks, DP_AXES, split_axis=0, concat_axis=1, tiled=True),
        SEQ_AXES,
        split_axis=1,
        concat_axis=1,
        tiled=True,
    )
    delta_blk = delta_head.reshape(query_blocks, BLOCK, heads_here, HEAD_DIM)
    prob_grad = jnp.concatenate(
        [
            jnp.einsum("bqhe,bkhe->bhqk", delta_blk, value_win, preferred_element_type=jnp.float32),
            jnp.einsum("bqhe,khe->bhqk", delta_blk, value_glob, preferred_element_type=jnp.float32),
        ],
        axis=-1,
    )
    keep_rows = (
        jnp.where(is_global, 0.0, 1.0).astype(jnp.float32).reshape(query_blocks, 1, BLOCK, 1)
    )
    score_bf = (
        prob_rows * (prob_grad - jnp.sum(prob_rows * prob_grad, axis=-1, keepdims=True)) * keep_rows
    ).astype(jnp.bfloat16)
    prob_kept = prob_bf * keep_rows.astype(jnp.bfloat16)
    grad_query = jnp.einsum(
        "bhqk,bkhe->bqhe", score_bf[..., :window_keys], key_win, preferred_element_type=jnp.float32
    )
    grad_query = (
        grad_query
        + jnp.einsum(
            "bhqk,khe->bqhe",
            score_bf[..., window_keys:],
            key_glob,
            preferred_element_type=jnp.float32,
        )
    ) * scaling
    flat_ids = block_ids.reshape(-1)
    key_part = (
        jnp.einsum(
            "bhqk,bqhe->bkhe",
            score_bf[..., :window_keys],
            query_blk,
            preferred_element_type=jnp.float32,
        )
        * scaling
    )
    key_globpart = (
        jnp.einsum(
            "bhqk,bqhe->khe",
            score_bf[..., window_keys:],
            query_blk,
            preferred_element_type=jnp.float32,
        )
        * scaling
    )
    value_part = jnp.einsum(
        "bhqk,bqhe->bkhe",
        prob_kept[..., :window_keys],
        delta_blk,
        preferred_element_type=jnp.float32,
    )
    value_globpart = jnp.einsum(
        "bhqk,bqhe->khe",
        prob_kept[..., window_keys:],
        delta_blk,
        preferred_element_type=jnp.float32,
    )
    block_hot = (block_ids[:, :, None] == jnp.arange(block_total, dtype=jnp.int32)).astype(
        jnp.float32
    )

    def place_blocks(parts):
        return jnp.einsum(
            "bjc,bjke->cke",
            block_hot,
            parts.reshape(query_blocks, 3 + RANDOM, BLOCK, columns),
            precision=lax.Precision.HIGHEST,
            preferred_element_type=jnp.float32,
        ).reshape(seq_length, columns)

    grad_key = place_blocks(key_part)
    grad_key = grad_key.at[doc_globals].add(key_globpart.reshape(global_count, columns))
    grad_value = place_blocks(value_part)
    grad_value = grad_value.at[doc_globals].add(value_globpart.reshape(global_count, columns))
    delta_glob = (
        jnp.einsum(
            "ng,nc->gc",
            picker,
            delta_head.reshape(query_count, columns),
            preferred_element_type=jnp.float32,
        )
        .astype(jnp.bfloat16)
        .reshape(global_count, heads_here, HEAD_DIM)
    )
    prob_grad_glob = jnp.einsum(
        "ghe,the->hgt", delta_glob, value_all, preferred_element_type=jnp.float32
    )
    score_glob_bf = (
        prob_glob * (prob_grad_glob - jnp.sum(prob_glob * prob_grad_glob, axis=-1, keepdims=True))
    ).astype(jnp.bfloat16)
    grad_query_glob = (
        jnp.einsum(
            "hgt,the->ghe", score_glob_bf, key_all, preferred_element_type=jnp.float32
        ).reshape(global_count, columns)
        * scaling
    )
    grad_key = (
        grad_key
        + jnp.einsum(
            "hgt,ghe->the", score_glob_bf, query_glob, preferred_element_type=jnp.float32
        ).reshape(seq_length, columns)
        * scaling
    )
    grad_value = grad_value + jnp.einsum(
        "hgt,ghe->the", prob_glob_bf, delta_glob, preferred_element_type=jnp.float32
    ).reshape(seq_length, columns)
    grad_query_all = grad_query.reshape(query_count, columns) + jnp.dot(
        picker_f, grad_query_glob, precision=lax.Precision.HIGHEST
    )
    def my_half(grads):
        halves = grads.reshape(seq_devices, splitting, slice_rows, columns)
        mine = jnp.where(my_slice == 0, halves[:, 0], halves[:, 1])
        theirs = jnp.where(my_slice == 0, halves[:, 1], halves[:, 0])
        received = lax.ppermute(theirs.astype(jnp.bfloat16), "sx", partner)
        return (mine + received.astype(jnp.float32)).astype(jnp.bfloat16)

    def to_positions(rows):
        back = lax.all_to_all(rows, SEQ_AXES, split_axis=0, concat_axis=0, tiled=True)
        return (
            back.reshape(head_groups, splitting, slice_rows, columns)
            .transpose(1, 2, 0, 3)
            .reshape(1, tokens, width)
        )

    grad_queries = to_positions(
        grad_query_all.astype(jnp.bfloat16).reshape(seq_devices, slice_rows, columns)
    )
    grad_keys = to_positions(my_half(grad_key))
    grad_values = to_positions(my_half(grad_value))
    return (grad_queries, grad_keys, grad_values, grad_out_proj)


def solution(mesh):
    seq_size, dp_size = mesh.shape["seq"], mesh.shape["dp"]
    torus = Mesh(
        mesh.devices.reshape(seq_size // 4, 4, dp_size // 2, 2), SEQ_AXES + DP_AXES
    )
    return jax.shard_map(
        shards,
        mesh=torus,
        in_specs=(
            P(DP_AXES, SEQ_AXES, None),
            P(DP_AXES, SEQ_AXES, None),
            P(DP_AXES, SEQ_AXES, None),
            P(DP_AXES, SEQ_AXES, None),
            P(DP_AXES, None, None),
            P(DP_AXES, None),
            P(DP_AXES, None),
        ),
        out_specs=(P(DP_AXES, SEQ_AXES, None), P(DP_AXES, SEQ_AXES, None), P(DP_AXES, SEQ_AXES, None), P(DP_AXES, None)),
        check_vma=False,
    )
```

```python
import math

import jax
import jax.numpy as jnp
from jax import lax
from jax.sharding import Mesh, PartitionSpec as P

HEAD_DIM = 128
BLOCK = 64
RANDOM = 3


MASKED = -1e30
SEQ_AXES = ("sz", "sx")
DP_AXES = ("dy", "dc")


def softmax_rows(scores):
    highest = jnp.max(scores, axis=-1, keepdims=True)
    raised = jnp.exp(scores - highest)
    return raised / jnp.sum(raised, axis=-1, keepdims=True)


def shards(query_rows, key_rows, value_rows, out_grad, rand_blocks, global_tokens, out_proj):
    seq_devices = lax.axis_size(SEQ_AXES)
    dp_devices = lax.axis_size(DP_AXES)
    tokens = query_rows.shape[1]
    width = query_rows.shape[2]
    model_width = out_grad.shape[2]
    head_count = width // HEAD_DIM
    splitting = max(seq_devices // head_count, 1)
    heads_here = max(head_count // seq_devices, 1)
    columns = heads_here * HEAD_DIM
    head_groups = seq_devices // splitting
    slice_rows = tokens // splitting
    seq_length = tokens * seq_devices
    block_total = seq_length // BLOCK
    window_keys = (3 + RANDOM) * BLOCK
    query_count = seq_devices * slice_rows
    query_blocks = query_count // BLOCK
    owned_groups = seq_devices // dp_devices // splitting
    global_count = global_tokens.shape[1]
    scaling = 1.0 / math.sqrt(HEAD_DIM)
    my_slice = lax.axis_index(SEQ_AXES) % splitting
    doc_blocks = rand_blocks[0]
    doc_globals = global_tokens[0]
    def head_rows(rows):
        return (
            rows[0]
            .reshape(splitting, slice_rows, head_groups, columns)
            .transpose(2, 0, 1, 3)
            .reshape(seq_devices, slice_rows, columns)
        )

    partner = [(i, i ^ 1) for i in range(lax.axis_size("sx"))]

    def both_halves(mine):
        other = lax.ppermute(mine, "sx", partner)
        low = jnp.where(my_slice == 0, mine, other)
        high = jnp.where(my_slice == 0, other, mine)
        return jnp.stack([low, high], axis=2).reshape(mine.shape[0], seq_devices, tokens, columns)

    head_parts = lax.all_to_all(
        jnp.stack([head_rows(query_rows), head_rows(key_rows), head_rows(value_rows)], axis=0),
        SEQ_AXES,
        split_axis=1,
        concat_axis=1,
        tiled=True,
    )
    query_head = head_parts[0]
    key_head, value_head = both_halves(head_parts[1:])
    source_start = jnp.arange(seq_devices, dtype=jnp.int32)[:, None] * tokens
    offsets = jnp.arange(slice_rows, dtype=jnp.int32)[None, :]
    query_pos = (source_start + my_slice * slice_rows + offsets).reshape(query_count)
    block_of = query_pos.reshape(query_blocks, BLOCK)[:, 0] // BLOCK
    window = block_of[:, None] + jnp.arange(-1, 2, dtype=jnp.int32)[None, :]
    inside = (window >= 0) & (window < block_total)
    block_ids = jnp.concatenate(
        [jnp.clip(window, 0, block_total - 1), jnp.take(doc_blocks, block_of, axis=0)], axis=1
    )
    usable = jnp.concatenate(
        [jnp.repeat(inside, BLOCK, axis=1), jnp.ones((query_blocks, RANDOM * BLOCK), dtype=bool)],
        axis=1,
    )
    key_all = key_head.reshape(seq_length, heads_here, HEAD_DIM)
    value_all = value_head.reshape(seq_length, heads_here, HEAD_DIM)
    key_win = key_all.reshape(block_total, BLOCK, heads_here, HEAD_DIM)[block_ids].reshape(
        query_blocks, window_keys, heads_here, HEAD_DIM
    )
    value_win = value_all.reshape(block_total, BLOCK, heads_here, HEAD_DIM)[block_ids].reshape(
        query_blocks, window_keys, heads_here, HEAD_DIM
    )
    key_glob = jnp.take(key_all, doc_globals, axis=0)
    value_glob = jnp.take(value_all, doc_globals, axis=0)
    query_blk = query_head.reshape(query_blocks, BLOCK, heads_here, HEAD_DIM)
    score_win = (
        jnp.einsum("bqhe,bkhe->bhqk", query_blk, key_win, preferred_element_type=jnp.float32)
        * scaling
    )
    score_win = jnp.where(usable[:, None, None, :], score_win, MASKED)
    score_glob = (
        jnp.einsum("bqhe,khe->bhqk", query_blk, key_glob, preferred_element_type=jnp.float32)
        * scaling
    )
    prob_rows = softmax_rows(jnp.concatenate([score_win, score_glob], axis=-1))
    prob_bf = prob_rows.astype(jnp.bfloat16)
    sparse_out = jnp.einsum(
        "bhqk,bkhe->bqhe", prob_bf[..., :window_keys], value_win, preferred_element_type=jnp.float32
    )
    sparse_out = sparse_out + jnp.einsum(
        "bhqk,khe->bqhe", prob_bf[..., window_keys:], value_glob, preferred_element_type=jnp.float32
    )
    matches = query_pos[:, None] == doc_globals[None, :]
    picker = matches.astype(jnp.bfloat16)
    picker_f = matches.astype(jnp.float32)
    is_global = jnp.any(matches, axis=1)
    query_glob = (
        jnp.einsum(
            "ng,nc->gc",
            picker,
            query_head.reshape(query_count, columns),
            preferred_element_type=jnp.float32,
        )
        .astype(jnp.bfloat16)
        .reshape(global_count, heads_here, HEAD_DIM)
    )
    prob_glob = softmax_rows(
        jnp.einsum("ghe,the->hgt", query_glob, key_all, preferred_element_type=jnp.float32)
        * scaling
    )
    prob_glob_bf = prob_glob.astype(jnp.bfloat16)
    glob_out = jnp.einsum(
        "hgt,the->ghe", prob_glob_bf, value_all, preferred_element_type=jnp.float32
    ).reshape(global_count, columns)
    placed = jnp.dot(picker_f, glob_out, precision=lax.Precision.HIGHEST)
    attention = jnp.where(
        is_global[:, None], placed, sparse_out.reshape(query_count, columns)
    ).astype(jnp.bfloat16)
    owned = lax.all_to_all(
        lax.all_to_all(
            attention.reshape(1, seq_devices, slice_rows, columns),
            SEQ_AXES,
            split_axis=1,
            concat_axis=1,
            tiled=True,
        ),
        DP_AXES,
        split_axis=1,
        concat_axis=0,
        tiled=True,
    )
    owned = owned.reshape(dp_devices, owned_groups, splitting, slice_rows, columns)
    proj_rows = out_proj.reshape(owned_groups, columns, model_width)
    piece_rows = lax.all_gather(out_grad, DP_AXES, axis=0, tiled=True)
    doc_count = piece_rows.shape[0]
    grads = piece_rows.reshape(doc_count, splitting, slice_rows, model_width)
    local_delta = jnp.einsum(
        "kptd,gcd->kgptc", grads, proj_rows, preferred_element_type=jnp.float32
    ).astype(jnp.bfloat16)
    local_delta = local_delta.reshape(doc_count, owned_groups * splitting, slice_rows, columns)
    delta_blocks = local_delta
    grad_sum = jnp.einsum("kgptc,kptd->gcd", owned, grads, preferred_element_type=jnp.float32)
    grad_sum, delta_blocks = (grad_sum, delta_blocks)
    z_size = lax.axis_size("sz")
    x_size = lax.axis_size("sx")
    proj_part = grad_sum.reshape(width // dp_devices, model_width).astype(jnp.bfloat16)
    z_rows = proj_part.shape[0] // (x_size * z_size)
    x_sum = jnp.sum(
        lax.all_to_all(
            proj_part.reshape(z_size, x_size, z_rows, model_width).transpose(1, 0, 2, 3),
            "sx",
            0,
            0,
            tiled=True,
        ).astype(jnp.float32),
        axis=0,
    )
    z_sum = jnp.sum(
        lax.all_to_all(
            x_sum.astype(jnp.bfloat16).reshape(z_size, z_rows, model_width), "sz", 0, 0, tiled=True
        ).astype(jnp.float32),
        axis=0,
    )
    grad_out_proj = lax.all_gather(z_sum.astype(jnp.bfloat16), SEQ_AXES, axis=0, tiled=True)
    delta_head = lax.all_to_all(
        lax.all_to_all(delta_blocks, DP_AXES, split_axis=0, concat_axis=1, tiled=True),
        SEQ_AXES,
        split_axis=1,
        concat_axis=1,
        tiled=True,
    )
    delta_blk = delta_head.reshape(query_blocks, BLOCK, heads_here, HEAD_DIM)
    prob_grad = jnp.concatenate(
        [
            jnp.einsum("bqhe,bkhe->bhqk", delta_blk, value_win, preferred_element_type=jnp.float32),
            jnp.einsum("bqhe,khe->bhqk", delta_blk, value_glob, preferred_element_type=jnp.float32),
        ],
        axis=-1,
    )
    keep_rows = (
        jnp.where(is_global, 0.0, 1.0).astype(jnp.float32).reshape(query_blocks, 1, BLOCK, 1)
    )
    score_bf = (
        prob_rows * (prob_grad - jnp.sum(prob_rows * prob_grad, axis=-1, keepdims=True)) * keep_rows
    ).astype(jnp.bfloat16)
    prob_kept = prob_bf * keep_rows.astype(jnp.bfloat16)
    grad_query = jnp.einsum(
        "bhqk,bkhe->bqhe", score_bf[..., :window_keys], key_win, preferred_element_type=jnp.float32
    )
    grad_query = (
        grad_query
        + jnp.einsum(
            "bhqk,khe->bqhe",
            score_bf[..., window_keys:],
            key_glob,
            preferred_element_type=jnp.float32,
        )
    ) * scaling
    flat_ids = block_ids.reshape(-1)
    key_part = (
        jnp.einsum(
            "bhqk,bqhe->bkhe",
            score_bf[..., :window_keys],
            query_blk,
            preferred_element_type=jnp.float32,
        )
        * scaling
    )
    key_globpart = (
        jnp.einsum(
            "bhqk,bqhe->khe",
            score_bf[..., window_keys:],
            query_blk,
            preferred_element_type=jnp.float32,
        )
        * scaling
    )
    value_part = jnp.einsum(
        "bhqk,bqhe->bkhe",
        prob_kept[..., :window_keys],
        delta_blk,
        preferred_element_type=jnp.float32,
    )
    value_globpart = jnp.einsum(
        "bhqk,bqhe->khe",
        prob_kept[..., window_keys:],
        delta_blk,
        preferred_element_type=jnp.float32,
    )
    block_hot = (block_ids[:, :, None] == jnp.arange(block_total, dtype=jnp.int32)).astype(
        jnp.float32
    )

    def place_blocks(parts):
        return jnp.einsum(
            "bjc,bjke->cke",
            block_hot,
            parts.reshape(query_blocks, 3 + RANDOM, BLOCK, columns),
            precision=lax.Precision.HIGHEST,
            preferred_element_type=jnp.float32,
        ).reshape(seq_length, columns)

    grad_key = place_blocks(key_part)
    grad_key = grad_key.at[doc_globals].add(key_globpart.reshape(global_count, columns))
    grad_value = place_blocks(value_part)
    grad_value = grad_value.at[doc_globals].add(value_globpart.reshape(global_count, columns))
    delta_glob = (
        jnp.einsum(
            "ng,nc->gc",
            picker,
            delta_head.reshape(query_count, columns),
            preferred_element_type=jnp.float32,
        )
        .astype(jnp.bfloat16)
        .reshape(global_count, heads_here, HEAD_DIM)
    )
    prob_grad_glob = jnp.einsum(
        "ghe,the->hgt", delta_glob, value_all, preferred_element_type=jnp.float32
    )
    score_glob_bf = (
        prob_glob * (prob_grad_glob - jnp.sum(prob_glob * prob_grad_glob, axis=-1, keepdims=True))
    ).astype(jnp.bfloat16)
    grad_query_glob = (
        jnp.einsum(
            "hgt,the->ghe", score_glob_bf, key_all, preferred_element_type=jnp.float32
        ).reshape(global_count, columns)
        * scaling
    )
    grad_key = (
        grad_key
        + jnp.einsum(
            "hgt,ghe->the", score_glob_bf, query_glob, preferred_element_type=jnp.float32
        ).reshape(seq_length, columns)
        * scaling
    )
    grad_value = grad_value + jnp.einsum(
        "hgt,ghe->the", prob_glob_bf, delta_glob, preferred_element_type=jnp.float32
    ).reshape(seq_length, columns)
    grad_query_all = grad_query.reshape(query_count, columns) + jnp.dot(
        picker_f, grad_query_glob, precision=lax.Precision.HIGHEST
    )
    halves = jnp.stack([grad_key, grad_value], axis=0).reshape(
        2, seq_devices, splitting, slice_rows, columns
    )
    mine = jnp.where(my_slice == 0, halves[:, :, 0], halves[:, :, 1])
    theirs = jnp.where(my_slice == 0, halves[:, :, 1], halves[:, :, 0])
    received = lax.ppermute(theirs.astype(jnp.bfloat16), "sx", partner)
    pair_sums = (mine + received.astype(jnp.float32)).astype(jnp.bfloat16)
    back = lax.all_to_all(
        jnp.concatenate(
            [
                grad_query_all.astype(jnp.bfloat16).reshape(1, seq_devices, slice_rows, columns),
                pair_sums,
            ],
            axis=0,
        ),
        SEQ_AXES,
        split_axis=1,
        concat_axis=1,
        tiled=True,
    )
    back = (
        back.reshape(3, head_groups, splitting, slice_rows, columns)
        .transpose(0, 2, 3, 1, 4)
        .reshape(3, 1, tokens, width)
    )
    grad_queries, grad_keys, grad_values = back[0], back[1], back[2]
    return (grad_queries, grad_keys, grad_values, grad_out_proj)


def solution(mesh):
    seq_size, dp_size = mesh.shape["seq"], mesh.shape["dp"]
    torus = Mesh(
        mesh.devices.reshape(seq_size // 4, 4, dp_size // 2, 2), SEQ_AXES + DP_AXES
    )
    return jax.shard_map(
        shards,
        mesh=torus,
        in_specs=(
            P(DP_AXES, SEQ_AXES, None),
            P(DP_AXES, SEQ_AXES, None),
            P(DP_AXES, SEQ_AXES, None),
            P(DP_AXES, SEQ_AXES, None),
            P(DP_AXES, None, None),
            P(DP_AXES, None),
            P(DP_AXES, None),
        ),
        out_specs=(P(DP_AXES, SEQ_AXES, None), P(DP_AXES, SEQ_AXES, None), P(DP_AXES, SEQ_AXES, None), P(DP_AXES, None)),
        check_vma=False,
    )
```

```python
import math

import jax
import jax.numpy as jnp
from jax import lax
from jax.sharding import Mesh, PartitionSpec as P

HEAD_DIM = 128
BLOCK = 64
RANDOM = 3


MASKED = -1e30
SEQ_AXES = ("sz", "sx")
DP_AXES = ("dy", "dc")


def softmax_rows(scores):
    highest = jnp.max(scores, axis=-1, keepdims=True)
    raised = jnp.exp(scores - highest)
    return raised / jnp.sum(raised, axis=-1, keepdims=True)


def shards(query_rows, key_rows, value_rows, out_grad, rand_blocks, global_tokens, out_proj):
    seq_devices = lax.axis_size(SEQ_AXES)
    dp_devices = lax.axis_size(DP_AXES)
    tokens = query_rows.shape[1]
    width = query_rows.shape[2]
    model_width = out_grad.shape[2]
    head_count = width // HEAD_DIM
    splitting = max(seq_devices // head_count, 1)
    heads_here = max(head_count // seq_devices, 1)
    columns = heads_here * HEAD_DIM
    head_groups = seq_devices // splitting
    slice_rows = tokens // splitting
    seq_length = tokens * seq_devices
    block_total = seq_length // BLOCK
    window_keys = (3 + RANDOM) * BLOCK
    query_count = seq_devices * slice_rows
    query_blocks = query_count // BLOCK
    owned_groups = seq_devices // dp_devices // splitting
    global_count = global_tokens.shape[1]
    scaling = 1.0 / math.sqrt(HEAD_DIM)
    my_slice = lax.axis_index(SEQ_AXES) % splitting
    doc_blocks = rand_blocks[0]
    doc_globals = global_tokens[0]
    def head_rows(rows):
        return (
            rows[0]
            .reshape(splitting, slice_rows, head_groups, columns)
            .transpose(2, 0, 1, 3)
            .reshape(seq_devices, slice_rows, columns)
        )

    partner = [(i, i ^ 1) for i in range(lax.axis_size("sx"))]

    def both_halves(mine):
        other = lax.ppermute(mine, "sx", partner)
        low = jnp.where(my_slice == 0, mine, other)
        high = jnp.where(my_slice == 0, other, mine)
        return jnp.stack([low, high], axis=2).reshape(mine.shape[0], seq_devices, tokens, columns)

    head_parts = lax.all_to_all(
        jnp.stack([head_rows(query_rows), head_rows(key_rows), head_rows(value_rows)], axis=0),
        SEQ_AXES,
        split_axis=1,
        concat_axis=1,
        tiled=True,
    )
    query_head = head_parts[0]
    key_head, value_head = both_halves(head_parts[1:])
    source_start = jnp.arange(seq_devices, dtype=jnp.int32)[:, None] * tokens
    offsets = jnp.arange(slice_rows, dtype=jnp.int32)[None, :]
    query_pos = (source_start + my_slice * slice_rows + offsets).reshape(query_count)
    block_of = query_pos.reshape(query_blocks, BLOCK)[:, 0] // BLOCK
    window = block_of[:, None] + jnp.arange(-1, 2, dtype=jnp.int32)[None, :]
    inside = (window >= 0) & (window < block_total)
    block_ids = jnp.concatenate(
        [jnp.clip(window, 0, block_total - 1), jnp.take(doc_blocks, block_of, axis=0)], axis=1
    )
    usable = jnp.concatenate(
        [jnp.repeat(inside, BLOCK, axis=1), jnp.ones((query_blocks, RANDOM * BLOCK), dtype=bool)],
        axis=1,
    )
    key_all = key_head.reshape(seq_length, heads_here, HEAD_DIM)
    value_all = value_head.reshape(seq_length, heads_here, HEAD_DIM)
    key_win = key_all.reshape(block_total, BLOCK, heads_here, HEAD_DIM)[block_ids].reshape(
        query_blocks, window_keys, heads_here, HEAD_DIM
    )
    value_win = value_all.reshape(block_total, BLOCK, heads_here, HEAD_DIM)[block_ids].reshape(
        query_blocks, window_keys, heads_here, HEAD_DIM
    )
    key_glob = jnp.take(key_all, doc_globals, axis=0)
    value_glob = jnp.take(value_all, doc_globals, axis=0)
    query_blk = query_head.reshape(query_blocks, BLOCK, heads_here, HEAD_DIM)
    score_win = (
        jnp.einsum("bqhe,bkhe->bhqk", query_blk, key_win, preferred_element_type=jnp.float32)
        * scaling
    )
    score_win = jnp.where(usable[:, None, None, :], score_win, MASKED)
    score_glob = (
        jnp.einsum("bqhe,khe->bhqk", query_blk, key_glob, preferred_element_type=jnp.float32)
        * scaling
    )
    prob_rows = softmax_rows(jnp.concatenate([score_win, score_glob], axis=-1))
    prob_bf = prob_rows.astype(jnp.bfloat16)
    sparse_out = jnp.einsum(
        "bhqk,bkhe->bqhe", prob_bf[..., :window_keys], value_win, preferred_element_type=jnp.float32
    )
    sparse_out = sparse_out + jnp.einsum(
        "bhqk,khe->bqhe", prob_bf[..., window_keys:], value_glob, preferred_element_type=jnp.float32
    )
    matches = query_pos[:, None] == doc_globals[None, :]
    picker = matches.astype(jnp.bfloat16)
    picker_f = matches.astype(jnp.float32)
    is_global = jnp.any(matches, axis=1)
    query_glob = (
        jnp.einsum(
            "ng,nc->gc",
            picker,
            query_head.reshape(query_count, columns),
            preferred_element_type=jnp.float32,
        )
        .astype(jnp.bfloat16)
        .reshape(global_count, heads_here, HEAD_DIM)
    )
    prob_glob = softmax_rows(
        jnp.einsum("ghe,the->hgt", query_glob, key_all, preferred_element_type=jnp.float32)
        * scaling
    )
    prob_glob_bf = prob_glob.astype(jnp.bfloat16)
    glob_out = jnp.einsum(
        "hgt,the->ghe", prob_glob_bf, value_all, preferred_element_type=jnp.float32
    ).reshape(global_count, columns)
    placed = jnp.dot(picker_f, glob_out, precision=lax.Precision.HIGHEST)
    attention = jnp.where(
        is_global[:, None], placed, sparse_out.reshape(query_count, columns)
    ).astype(jnp.bfloat16)
    owned = lax.all_to_all(
        lax.all_to_all(
            attention.reshape(1, seq_devices, slice_rows, columns),
            SEQ_AXES,
            split_axis=1,
            concat_axis=1,
            tiled=True,
        ),
        DP_AXES,
        split_axis=1,
        concat_axis=0,
        tiled=True,
    )
    owned = owned.reshape(dp_devices, owned_groups, splitting, slice_rows, columns)
    proj_rows = out_proj.reshape(owned_groups, columns, model_width)
    piece_rows = lax.all_gather(out_grad, DP_AXES, axis=0, tiled=True)
    doc_count = piece_rows.shape[0]
    grads = piece_rows.reshape(doc_count, splitting, slice_rows, model_width)
    local_delta = jnp.einsum(
        "kptd,gcd->kgptc", grads, proj_rows, preferred_element_type=jnp.float32
    ).astype(jnp.bfloat16)
    local_delta = local_delta.reshape(doc_count, owned_groups * splitting, slice_rows, columns)
    delta_blocks = local_delta
    grad_sum = jnp.einsum("kgptc,kptd->gcd", owned, grads, preferred_element_type=jnp.float32)
    grad_sum, delta_blocks = (grad_sum, delta_blocks)
    z_size = lax.axis_size("sz")
    x_size = lax.axis_size("sx")
    proj_part = grad_sum.reshape(width // dp_devices, model_width).astype(jnp.bfloat16)
    z_rows = proj_part.shape[0] // (x_size * z_size)
    x_sum = jnp.sum(
        lax.all_to_all(
            proj_part.reshape(z_size, x_size, z_rows, model_width).transpose(1, 0, 2, 3),
            "sx",
            0,
            0,
            tiled=True,
        ).astype(jnp.float32),
        axis=0,
    )
    z_sum = jnp.sum(
        lax.all_to_all(
            x_sum.astype(jnp.bfloat16).reshape(z_size, z_rows, model_width), "sz", 0, 0, tiled=True
        ).astype(jnp.float32),
        axis=0,
    )
    z_sum, delta_blocks = lax.optimization_barrier((z_sum, delta_blocks))
    grad_out_proj = lax.all_gather(z_sum.astype(jnp.bfloat16), SEQ_AXES, axis=0, tiled=True)
    delta_head = lax.all_to_all(
        lax.all_to_all(delta_blocks, DP_AXES, split_axis=0, concat_axis=1, tiled=True),
        SEQ_AXES,
        split_axis=1,
        concat_axis=1,
        tiled=True,
    )
    delta_blk = delta_head.reshape(query_blocks, BLOCK, heads_here, HEAD_DIM)
    prob_grad = jnp.concatenate(
        [
            jnp.einsum("bqhe,bkhe->bhqk", delta_blk, value_win, preferred_element_type=jnp.float32),
            jnp.einsum("bqhe,khe->bhqk", delta_blk, value_glob, preferred_element_type=jnp.float32),
        ],
        axis=-1,
    )
    keep_rows = (
        jnp.where(is_global, 0.0, 1.0).astype(jnp.float32).reshape(query_blocks, 1, BLOCK, 1)
    )
    score_bf = (
        prob_rows * (prob_grad - jnp.sum(prob_rows * prob_grad, axis=-1, keepdims=True)) * keep_rows
    ).astype(jnp.bfloat16)
    prob_kept = prob_bf * keep_rows.astype(jnp.bfloat16)
    grad_query = jnp.einsum(
        "bhqk,bkhe->bqhe", score_bf[..., :window_keys], key_win, preferred_element_type=jnp.float32
    )
    grad_query = (
        grad_query
        + jnp.einsum(
            "bhqk,khe->bqhe",
            score_bf[..., window_keys:],
            key_glob,
            preferred_element_type=jnp.float32,
        )
    ) * scaling
    flat_ids = block_ids.reshape(-1)
    key_part = (
        jnp.einsum(
            "bhqk,bqhe->bkhe",
            score_bf[..., :window_keys],
            query_blk,
            preferred_element_type=jnp.float32,
        )
        * scaling
    )
    key_globpart = (
        jnp.einsum(
            "bhqk,bqhe->khe",
            score_bf[..., window_keys:],
            query_blk,
            preferred_element_type=jnp.float32,
        )
        * scaling
    )
    value_part = jnp.einsum(
        "bhqk,bqhe->bkhe",
        prob_kept[..., :window_keys],
        delta_blk,
        preferred_element_type=jnp.float32,
    )
    value_globpart = jnp.einsum(
        "bhqk,bqhe->khe",
        prob_kept[..., window_keys:],
        delta_blk,
        preferred_element_type=jnp.float32,
    )
    block_hot = (block_ids[:, :, None] == jnp.arange(block_total, dtype=jnp.int32)).astype(
        jnp.float32
    )

    def place_blocks(parts):
        return jnp.einsum(
            "bjc,bjke->cke",
            block_hot,
            parts.reshape(query_blocks, 3 + RANDOM, BLOCK, columns),
            precision=lax.Precision.HIGHEST,
            preferred_element_type=jnp.float32,
        ).reshape(seq_length, columns)

    grad_key = place_blocks(key_part)
    grad_key = grad_key.at[doc_globals].add(key_globpart.reshape(global_count, columns))
    grad_value = place_blocks(value_part)
    grad_value = grad_value.at[doc_globals].add(value_globpart.reshape(global_count, columns))
    delta_glob = (
        jnp.einsum(
            "ng,nc->gc",
            picker,
            delta_head.reshape(query_count, columns),
            preferred_element_type=jnp.float32,
        )
        .astype(jnp.bfloat16)
        .reshape(global_count, heads_here, HEAD_DIM)
    )
    prob_grad_glob = jnp.einsum(
        "ghe,the->hgt", delta_glob, value_all, preferred_element_type=jnp.float32
    )
    score_glob_bf = (
        prob_glob * (prob_grad_glob - jnp.sum(prob_glob * prob_grad_glob, axis=-1, keepdims=True))
    ).astype(jnp.bfloat16)
    grad_query_glob = (
        jnp.einsum(
            "hgt,the->ghe", score_glob_bf, key_all, preferred_element_type=jnp.float32
        ).reshape(global_count, columns)
        * scaling
    )
    grad_key = (
        grad_key
        + jnp.einsum(
            "hgt,ghe->the", score_glob_bf, query_glob, preferred_element_type=jnp.float32
        ).reshape(seq_length, columns)
        * scaling
    )
    grad_value = grad_value + jnp.einsum(
        "hgt,ghe->the", prob_glob_bf, delta_glob, preferred_element_type=jnp.float32
    ).reshape(seq_length, columns)
    grad_query_all = grad_query.reshape(query_count, columns) + jnp.dot(
        picker_f, grad_query_glob, precision=lax.Precision.HIGHEST
    )
    halves = jnp.stack([grad_key, grad_value], axis=0).reshape(
        2, seq_devices, splitting, slice_rows, columns
    )
    mine = jnp.where(my_slice == 0, halves[:, :, 0], halves[:, :, 1])
    theirs = jnp.where(my_slice == 0, halves[:, :, 1], halves[:, :, 0])
    received = lax.ppermute(theirs.astype(jnp.bfloat16), "sx", partner)
    pair_sums = (mine + received.astype(jnp.float32)).astype(jnp.bfloat16)
    back = lax.all_to_all(
        jnp.concatenate(
            [
                grad_query_all.astype(jnp.bfloat16).reshape(1, seq_devices, slice_rows, columns),
                pair_sums,
            ],
            axis=0,
        ),
        SEQ_AXES,
        split_axis=1,
        concat_axis=1,
        tiled=True,
    )
    back = (
        back.reshape(3, head_groups, splitting, slice_rows, columns)
        .transpose(0, 2, 3, 1, 4)
        .reshape(3, 1, tokens, width)
    )
    grad_queries, grad_keys, grad_values = back[0], back[1], back[2]
    return (grad_queries, grad_keys, grad_values, grad_out_proj)


def solution(mesh):
    seq_size, dp_size = mesh.shape["seq"], mesh.shape["dp"]
    torus = Mesh(
        mesh.devices.reshape(seq_size // 4, 4, dp_size // 2, 2), SEQ_AXES + DP_AXES
    )
    return jax.shard_map(
        shards,
        mesh=torus,
        in_specs=(
            P(DP_AXES, SEQ_AXES, None),
            P(DP_AXES, SEQ_AXES, None),
            P(DP_AXES, SEQ_AXES, None),
            P(DP_AXES, SEQ_AXES, None),
            P(DP_AXES, None, None),
            P(DP_AXES, None),
            P(DP_AXES, None),
        ),
        out_specs=(P(DP_AXES, SEQ_AXES, None), P(DP_AXES, SEQ_AXES, None), P(DP_AXES, SEQ_AXES, None), P(DP_AXES, None)),
        check_vma=False,
    )
```

```python
import math

import jax
import jax.numpy as jnp
from jax import lax
from jax.sharding import Mesh, PartitionSpec as P

HEAD_DIM = 128
BLOCK = 64
RANDOM = 3


MASKED = -1e30
SEQ_AXES = ("sz", "sx")
DP_AXES = ("dy", "dc")


def softmax_rows(scores):
    highest = jnp.max(scores, axis=-1, keepdims=True)
    raised = jnp.exp(scores - highest)
    return raised / jnp.sum(raised, axis=-1, keepdims=True)


def shards(query_rows, key_rows, value_rows, out_grad, rand_blocks, global_tokens, out_proj):
    seq_devices = lax.axis_size(SEQ_AXES)
    dp_devices = lax.axis_size(DP_AXES)
    tokens = query_rows.shape[1]
    width = query_rows.shape[2]
    model_width = out_grad.shape[2]
    head_count = width // HEAD_DIM
    splitting = max(seq_devices // head_count, 1)
    heads_here = max(head_count // seq_devices, 1)
    columns = heads_here * HEAD_DIM
    head_groups = seq_devices // splitting
    slice_rows = tokens // splitting
    seq_length = tokens * seq_devices
    block_total = seq_length // BLOCK
    window_keys = (3 + RANDOM) * BLOCK
    query_count = seq_devices * slice_rows
    query_blocks = query_count // BLOCK
    owned_groups = seq_devices // dp_devices // splitting
    global_count = global_tokens.shape[1]
    scaling = 1.0 / math.sqrt(HEAD_DIM)
    my_slice = lax.axis_index(SEQ_AXES) % splitting
    doc_blocks = rand_blocks[0]
    doc_globals = global_tokens[0]
    def head_rows(rows):
        return (
            rows[0]
            .reshape(splitting, slice_rows, head_groups, columns)
            .transpose(2, 0, 1, 3)
            .reshape(seq_devices, slice_rows, columns)
        )

    partner = [(i, i ^ 1) for i in range(lax.axis_size("sx"))]

    def both_halves(mine):
        other = lax.ppermute(mine, "sx", partner)
        low = jnp.where(my_slice == 0, mine, other)
        high = jnp.where(my_slice == 0, other, mine)
        return jnp.stack([low, high], axis=1).reshape(seq_devices, tokens, columns)

    def to_heads(rows):
        return lax.all_to_all(head_rows(rows), SEQ_AXES, split_axis=0, concat_axis=0, tiled=True)

    query_head = to_heads(query_rows)
    key_head = both_halves(to_heads(key_rows))
    value_head = both_halves(to_heads(value_rows))
    source_start = jnp.arange(seq_devices, dtype=jnp.int32)[:, None] * tokens
    offsets = jnp.arange(slice_rows, dtype=jnp.int32)[None, :]
    query_pos = (source_start + my_slice * slice_rows + offsets).reshape(query_count)
    block_of = query_pos.reshape(query_blocks, BLOCK)[:, 0] // BLOCK
    window = block_of[:, None] + jnp.arange(-1, 2, dtype=jnp.int32)[None, :]
    inside = (window >= 0) & (window < block_total)
    block_ids = jnp.concatenate(
        [jnp.clip(window, 0, block_total - 1), jnp.take(doc_blocks, block_of, axis=0)], axis=1
    )
    usable = jnp.concatenate(
        [jnp.repeat(inside, BLOCK, axis=1), jnp.ones((query_blocks, RANDOM * BLOCK), dtype=bool)],
        axis=1,
    )
    key_all = key_head.reshape(seq_length, heads_here, HEAD_DIM)
    value_all = value_head.reshape(seq_length, heads_here, HEAD_DIM)
    key_win = key_all.reshape(block_total, BLOCK, heads_here, HEAD_DIM)[block_ids].reshape(
        query_blocks, window_keys, heads_here, HEAD_DIM
    )
    value_win = value_all.reshape(block_total, BLOCK, heads_here, HEAD_DIM)[block_ids].reshape(
        query_blocks, window_keys, heads_here, HEAD_DIM
    )
    key_glob = jnp.take(key_all, doc_globals, axis=0)
    value_glob = jnp.take(value_all, doc_globals, axis=0)
    query_blk = query_head.reshape(query_blocks, BLOCK, heads_here, HEAD_DIM)
    score_win = (
        jnp.einsum("bqhe,bkhe->bhqk", query_blk, key_win, preferred_element_type=jnp.float32)
        * scaling
    )
    score_win = jnp.where(usable[:, None, None, :], score_win, MASKED)
    score_glob = (
        jnp.einsum("bqhe,khe->bhqk", query_blk, key_glob, preferred_element_type=jnp.float32)
        * scaling
    )
    prob_rows = softmax_rows(jnp.concatenate([score_win, score_glob], axis=-1))
    prob_bf = prob_rows.astype(jnp.bfloat16)
    sparse_out = jnp.einsum(
        "bhqk,bkhe->bqhe", prob_bf[..., :window_keys], value_win, preferred_element_type=jnp.float32
    )
    sparse_out = sparse_out + jnp.einsum(
        "bhqk,khe->bqhe", prob_bf[..., window_keys:], value_glob, preferred_element_type=jnp.float32
    )
    matches = query_pos[:, None] == doc_globals[None, :]
    picker = matches.astype(jnp.bfloat16)
    picker_f = matches.astype(jnp.float32)
    is_global = jnp.any(matches, axis=1)
    query_glob = (
        jnp.einsum(
            "ng,nc->gc",
            picker,
            query_head.reshape(query_count, columns),
            preferred_element_type=jnp.float32,
        )
        .astype(jnp.bfloat16)
        .reshape(global_count, heads_here, HEAD_DIM)
    )
    prob_glob = softmax_rows(
        jnp.einsum("ghe,the->hgt", query_glob, key_all, preferred_element_type=jnp.float32)
        * scaling
    )
    prob_glob_bf = prob_glob.astype(jnp.bfloat16)
    glob_out = jnp.einsum(
        "hgt,the->ghe", prob_glob_bf, value_all, preferred_element_type=jnp.float32
    ).reshape(global_count, columns)
    placed = jnp.dot(picker_f, glob_out, precision=lax.Precision.HIGHEST)
    attention = jnp.where(
        is_global[:, None], placed, sparse_out.reshape(query_count, columns)
    ).astype(jnp.bfloat16)
    owned = lax.all_to_all(
        lax.all_to_all(
            attention.reshape(1, seq_devices, slice_rows, columns),
            SEQ_AXES,
            split_axis=1,
            concat_axis=1,
            tiled=True,
        ),
        DP_AXES,
        split_axis=1,
        concat_axis=0,
        tiled=True,
    )
    owned = owned.reshape(dp_devices, owned_groups, splitting, slice_rows, columns)
    proj_rows = out_proj.reshape(owned_groups, columns, model_width)
    piece_rows = lax.all_gather(out_grad, DP_AXES, axis=0, tiled=True)
    doc_count = piece_rows.shape[0]
    grads = piece_rows.reshape(doc_count, splitting, slice_rows, model_width)
    local_delta = jnp.einsum(
        "kptd,gcd->kgptc", grads, proj_rows, preferred_element_type=jnp.float32
    ).astype(jnp.bfloat16)
    local_delta = local_delta.reshape(doc_count, owned_groups * splitting, slice_rows, columns)
    delta_blocks = local_delta
    grad_sum = jnp.einsum("kgptc,kptd->gcd", owned, grads, preferred_element_type=jnp.float32)
    grad_sum, delta_blocks = (grad_sum, delta_blocks)
    z_size = lax.axis_size("sz")
    x_size = lax.axis_size("sx")
    proj_part = grad_sum.reshape(width // dp_devices, model_width).astype(jnp.bfloat16)
    z_rows = proj_part.shape[0] // (x_size * z_size)
    x_sum = jnp.sum(
        lax.all_to_all(
            proj_part.reshape(z_size, x_size, z_rows, model_width).transpose(1, 0, 2, 3),
            "sx",
            0,
            0,
            tiled=True,
        ).astype(jnp.float32),
        axis=0,
    )
    z_sum = jnp.sum(
        lax.all_to_all(
            x_sum.astype(jnp.bfloat16).reshape(z_size, z_rows, model_width), "sz", 0, 0, tiled=True
        ).astype(jnp.float32),
        axis=0,
    )
    grad_out_proj = lax.all_gather(z_sum.astype(jnp.bfloat16), SEQ_AXES, axis=0, tiled=True)
    delta_head = lax.all_to_all(
        lax.all_to_all(delta_blocks, DP_AXES, split_axis=0, concat_axis=1, tiled=True),
        SEQ_AXES,
        split_axis=1,
        concat_axis=1,
        tiled=True,
    )
    delta_blk = delta_head.reshape(query_blocks, BLOCK, heads_here, HEAD_DIM)
    prob_grad = jnp.concatenate(
        [
            jnp.einsum("bqhe,bkhe->bhqk", delta_blk, value_win, preferred_element_type=jnp.float32),
            jnp.einsum("bqhe,khe->bhqk", delta_blk, value_glob, preferred_element_type=jnp.float32),
        ],
        axis=-1,
    )
    keep_rows = (
        jnp.where(is_global, 0.0, 1.0).astype(jnp.float32).reshape(query_blocks, 1, BLOCK, 1)
    )
    score_bf = (
        prob_rows * (prob_grad - jnp.sum(prob_rows * prob_grad, axis=-1, keepdims=True)) * keep_rows
    ).astype(jnp.bfloat16)
    prob_kept = prob_bf * keep_rows.astype(jnp.bfloat16)
    grad_query = jnp.einsum(
        "bhqk,bkhe->bqhe", score_bf[..., :window_keys], key_win, preferred_element_type=jnp.float32
    )
    grad_query = (
        grad_query
        + jnp.einsum(
            "bhqk,khe->bqhe",
            score_bf[..., window_keys:],
            key_glob,
            preferred_element_type=jnp.float32,
        )
    ) * scaling
    flat_ids = block_ids.reshape(-1)
    window_blocks = (query_blocks, heads_here, BLOCK, 3 + RANDOM, BLOCK)
    key_part = (
        jnp.einsum(
            "bhqjk,bqhe->bjkhe",
            score_bf[..., :window_keys].reshape(window_blocks),
            query_blk,
            preferred_element_type=jnp.float32,
        )
        * scaling
    )
    key_globpart = (
        jnp.einsum(
            "bhqk,bqhe->khe",
            score_bf[..., window_keys:],
            query_blk,
            preferred_element_type=jnp.float32,
        )
        * scaling
    )
    value_part = jnp.einsum(
        "bhqjk,bqhe->bjkhe",
        prob_kept[..., :window_keys].reshape(window_blocks),
        delta_blk,
        preferred_element_type=jnp.float32,
    )
    value_globpart = jnp.einsum(
        "bhqk,bqhe->khe",
        prob_kept[..., window_keys:],
        delta_blk,
        preferred_element_type=jnp.float32,
    )
    block_hot = (block_ids[:, :, None] == jnp.arange(block_total, dtype=jnp.int32)).astype(
        jnp.float32
    )

    def place_blocks(parts):
        return jnp.einsum(
            "bjc,bjke->cke",
            block_hot,
            parts.reshape(query_blocks, 3 + RANDOM, BLOCK, columns),
            precision=lax.Precision.HIGH,
            preferred_element_type=jnp.float32,
        ).reshape(seq_length, columns)

    grad_key = place_blocks(key_part)
    grad_key = grad_key.at[doc_globals].add(key_globpart.reshape(global_count, columns))
    grad_value = place_blocks(value_part)
    grad_value = grad_value.at[doc_globals].add(value_globpart.reshape(global_count, columns))
    delta_glob = (
        jnp.einsum(
            "ng,nc->gc",
            picker,
            delta_head.reshape(query_count, columns),
            preferred_element_type=jnp.float32,
        )
        .astype(jnp.bfloat16)
        .reshape(global_count, heads_here, HEAD_DIM)
    )
    prob_grad_glob = jnp.einsum(
        "ghe,the->hgt", delta_glob, value_all, preferred_element_type=jnp.float32
    )
    score_glob_bf = (
        prob_glob * (prob_grad_glob - jnp.sum(prob_glob * prob_grad_glob, axis=-1, keepdims=True))
    ).astype(jnp.bfloat16)
    grad_query_glob = (
        jnp.einsum(
            "hgt,the->ghe", score_glob_bf, key_all, preferred_element_type=jnp.float32
        ).reshape(global_count, columns)
        * scaling
    )
    grad_key = (
        grad_key
        + jnp.einsum(
            "hgt,ghe->the", score_glob_bf, query_glob, preferred_element_type=jnp.float32
        ).reshape(seq_length, columns)
        * scaling
    )
    grad_value = grad_value + jnp.einsum(
        "hgt,ghe->the", prob_glob_bf, delta_glob, preferred_element_type=jnp.float32
    ).reshape(seq_length, columns)
    grad_query_all = grad_query.reshape(query_count, columns) + jnp.dot(
        picker_f, grad_query_glob, precision=lax.Precision.HIGHEST
    )
    def my_half(grads):
        halves = grads.reshape(seq_devices, splitting, slice_rows, columns)
        mine = jnp.where(my_slice == 0, halves[:, 0], halves[:, 1])
        theirs = jnp.where(my_slice == 0, halves[:, 1], halves[:, 0])
        received = lax.ppermute(theirs.astype(jnp.bfloat16), "sx", partner)
        return (mine + received.astype(jnp.float32)).astype(jnp.bfloat16)

    def to_positions(rows):
        back = lax.all_to_all(rows, SEQ_AXES, split_axis=0, concat_axis=0, tiled=True)
        return (
            back.reshape(head_groups, splitting, slice_rows, columns)
            .transpose(1, 2, 0, 3)
            .reshape(1, tokens, width)
        )

    grad_queries = to_positions(
        grad_query_all.astype(jnp.bfloat16).reshape(seq_devices, slice_rows, columns)
    )
    grad_keys = to_positions(my_half(grad_key))
    grad_values = to_positions(my_half(grad_value))
    return (grad_queries, grad_keys, grad_values, grad_out_proj)


def solution(mesh):
    seq_size, dp_size = mesh.shape["seq"], mesh.shape["dp"]
    torus = Mesh(
        mesh.devices.reshape(seq_size // 4, 4, dp_size // 2, 2), SEQ_AXES + DP_AXES
    )
    return jax.shard_map(
        shards,
        mesh=torus,
        in_specs=(
            P(DP_AXES, SEQ_AXES, None),
            P(DP_AXES, SEQ_AXES, None),
            P(DP_AXES, SEQ_AXES, None),
            P(DP_AXES, SEQ_AXES, None),
            P(DP_AXES, None, None),
            P(DP_AXES, None),
            P(DP_AXES, None),
        ),
        out_specs=(P(DP_AXES, SEQ_AXES, None), P(DP_AXES, SEQ_AXES, None), P(DP_AXES, SEQ_AXES, None), P(DP_AXES, None)),
        check_vma=False,
    )
```

```python
import math

import jax
import jax.numpy as jnp
from jax import lax
from jax.sharding import Mesh, PartitionSpec as P

HEAD_DIM = 128
BLOCK = 64
RANDOM = 3


MASKED = -1e30
SEQ_AXES = ("sz", "sx")
DP_AXES = ("dy", "dc")


def softmax_rows(scores):
    highest = jnp.max(scores, axis=-1, keepdims=True)
    raised = jnp.exp(scores - highest)
    return raised / jnp.sum(raised, axis=-1, keepdims=True)


def shards(query_rows, key_rows, value_rows, out_grad, rand_blocks, global_tokens, out_proj):
    seq_devices = lax.axis_size(SEQ_AXES)
    dp_devices = lax.axis_size(DP_AXES)
    tokens = query_rows.shape[1]
    width = query_rows.shape[2]
    model_width = out_grad.shape[2]
    head_count = width // HEAD_DIM
    splitting = max(seq_devices // head_count, 1)
    heads_here = max(head_count // seq_devices, 1)
    columns = heads_here * HEAD_DIM
    head_groups = seq_devices // splitting
    slice_rows = tokens // splitting
    seq_length = tokens * seq_devices
    block_total = seq_length // BLOCK
    window_keys = (3 + RANDOM) * BLOCK
    query_count = seq_devices * slice_rows
    query_blocks = query_count // BLOCK
    owned_groups = seq_devices // dp_devices // splitting
    global_count = global_tokens.shape[1]
    scaling = 1.0 / math.sqrt(HEAD_DIM)
    my_slice = lax.axis_index(SEQ_AXES) % splitting
    doc_blocks = rand_blocks[0]
    doc_globals = global_tokens[0]
    def head_rows(rows):
        return (
            rows[0]
            .reshape(splitting, slice_rows, head_groups, columns)
            .transpose(2, 0, 1, 3)
            .reshape(seq_devices, slice_rows, columns)
        )

    partner = [(i, i ^ 1) for i in range(lax.axis_size("sx"))]

    def both_halves(mine):
        other = lax.ppermute(mine, "sx", partner)
        low = jnp.where(my_slice == 0, mine, other)
        high = jnp.where(my_slice == 0, other, mine)
        return jnp.stack([low, high], axis=1).reshape(seq_devices, tokens, columns)

    def to_heads(rows):
        return lax.all_to_all(head_rows(rows), SEQ_AXES, split_axis=0, concat_axis=0, tiled=True)

    query_head = to_heads(query_rows)
    key_head = both_halves(to_heads(key_rows))
    value_head = both_halves(to_heads(value_rows))
    proj_rows = out_proj.reshape(owned_groups, columns, model_width)
    piece_rows = lax.all_gather(out_grad, DP_AXES, axis=0, tiled=True)
    doc_count = piece_rows.shape[0]
    grads = piece_rows.reshape(doc_count, splitting, slice_rows, model_width)
    local_delta = jnp.einsum(
        "kptd,gcd->kgptc", grads, proj_rows, preferred_element_type=jnp.float32
    ).astype(jnp.bfloat16)
    local_delta = local_delta.reshape(doc_count, owned_groups * splitting, slice_rows, columns)
    delta_blocks = local_delta
    delta_dp = lax.all_to_all(delta_blocks, DP_AXES, split_axis=0, concat_axis=1, tiled=True)
    delta_dp, query_head, key_head, value_head = lax.optimization_barrier(
        (delta_dp, query_head, key_head, value_head)
    )
    source_start = jnp.arange(seq_devices, dtype=jnp.int32)[:, None] * tokens
    offsets = jnp.arange(slice_rows, dtype=jnp.int32)[None, :]
    query_pos = (source_start + my_slice * slice_rows + offsets).reshape(query_count)
    block_of = query_pos.reshape(query_blocks, BLOCK)[:, 0] // BLOCK
    window = block_of[:, None] + jnp.arange(-1, 2, dtype=jnp.int32)[None, :]
    inside = (window >= 0) & (window < block_total)
    block_ids = jnp.concatenate(
        [jnp.clip(window, 0, block_total - 1), jnp.take(doc_blocks, block_of, axis=0)], axis=1
    )
    usable = jnp.concatenate(
        [jnp.repeat(inside, BLOCK, axis=1), jnp.ones((query_blocks, RANDOM * BLOCK), dtype=bool)],
        axis=1,
    )
    key_all = key_head.reshape(seq_length, heads_here, HEAD_DIM)
    value_all = value_head.reshape(seq_length, heads_here, HEAD_DIM)
    key_win = key_all.reshape(block_total, BLOCK, heads_here, HEAD_DIM)[block_ids].reshape(
        query_blocks, window_keys, heads_here, HEAD_DIM
    )
    value_win = value_all.reshape(block_total, BLOCK, heads_here, HEAD_DIM)[block_ids].reshape(
        query_blocks, window_keys, heads_here, HEAD_DIM
    )
    key_glob = jnp.take(key_all, doc_globals, axis=0)
    value_glob = jnp.take(value_all, doc_globals, axis=0)
    query_blk = query_head.reshape(query_blocks, BLOCK, heads_here, HEAD_DIM)
    score_win = (
        jnp.einsum("bqhe,bkhe->bhqk", query_blk, key_win, preferred_element_type=jnp.float32)
        * scaling
    )
    score_win = jnp.where(usable[:, None, None, :], score_win, MASKED)
    score_glob = (
        jnp.einsum("bqhe,khe->bhqk", query_blk, key_glob, preferred_element_type=jnp.float32)
        * scaling
    )
    prob_rows = softmax_rows(jnp.concatenate([score_win, score_glob], axis=-1))
    prob_bf = prob_rows.astype(jnp.bfloat16)
    sparse_out = jnp.einsum(
        "bhqk,bkhe->bqhe", prob_bf[..., :window_keys], value_win, preferred_element_type=jnp.float32
    )
    sparse_out = sparse_out + jnp.einsum(
        "bhqk,khe->bqhe", prob_bf[..., window_keys:], value_glob, preferred_element_type=jnp.float32
    )
    matches = query_pos[:, None] == doc_globals[None, :]
    picker = matches.astype(jnp.bfloat16)
    picker_f = matches.astype(jnp.float32)
    is_global = jnp.any(matches, axis=1)
    query_glob = (
        jnp.einsum(
            "ng,nc->gc",
            picker,
            query_head.reshape(query_count, columns),
            preferred_element_type=jnp.float32,
        )
        .astype(jnp.bfloat16)
        .reshape(global_count, heads_here, HEAD_DIM)
    )
    prob_glob = softmax_rows(
        jnp.einsum("ghe,the->hgt", query_glob, key_all, preferred_element_type=jnp.float32)
        * scaling
    )
    prob_glob_bf = prob_glob.astype(jnp.bfloat16)
    glob_out = jnp.einsum(
        "hgt,the->ghe", prob_glob_bf, value_all, preferred_element_type=jnp.float32
    ).reshape(global_count, columns)
    placed = jnp.dot(picker_f, glob_out, precision=lax.Precision.HIGHEST)
    attention = jnp.where(
        is_global[:, None], placed, sparse_out.reshape(query_count, columns)
    ).astype(jnp.bfloat16)
    owned = lax.all_to_all(
        lax.all_to_all(
            attention.reshape(1, seq_devices, slice_rows, columns),
            SEQ_AXES,
            split_axis=1,
            concat_axis=1,
            tiled=True,
        ),
        DP_AXES,
        split_axis=1,
        concat_axis=0,
        tiled=True,
    )
    owned = owned.reshape(dp_devices, owned_groups, splitting, slice_rows, columns)
    grad_sum = jnp.einsum("kgptc,kptd->gcd", owned, grads, preferred_element_type=jnp.float32)
    grad_sum, delta_blocks = (grad_sum, delta_blocks)
    z_size = lax.axis_size("sz")
    x_size = lax.axis_size("sx")
    proj_part = grad_sum.reshape(width // dp_devices, model_width).astype(jnp.bfloat16)
    z_rows = proj_part.shape[0] // (x_size * z_size)
    x_sum = jnp.sum(
        lax.all_to_all(
            proj_part.reshape(z_size, x_size, z_rows, model_width).transpose(1, 0, 2, 3),
            "sx",
            0,
            0,
            tiled=True,
        ).astype(jnp.float32),
        axis=0,
    )
    z_sum = jnp.sum(
        lax.all_to_all(
            x_sum.astype(jnp.bfloat16).reshape(z_size, z_rows, model_width), "sz", 0, 0, tiled=True
        ).astype(jnp.float32),
        axis=0,
    )
    grad_out_proj = lax.all_gather(z_sum.astype(jnp.bfloat16), SEQ_AXES, axis=0, tiled=True)
    delta_head = lax.all_to_all(
        delta_dp,
        SEQ_AXES,
        split_axis=1,
        concat_axis=1,
        tiled=True,
    )
    delta_blk = delta_head.reshape(query_blocks, BLOCK, heads_here, HEAD_DIM)
    prob_grad = jnp.concatenate(
        [
            jnp.einsum("bqhe,bkhe->bhqk", delta_blk, value_win, preferred_element_type=jnp.float32),
            jnp.einsum("bqhe,khe->bhqk", delta_blk, value_glob, preferred_element_type=jnp.float32),
        ],
        axis=-1,
    )
    keep_rows = (
        jnp.where(is_global, 0.0, 1.0).astype(jnp.float32).reshape(query_blocks, 1, BLOCK, 1)
    )
    score_bf = (
        prob_rows * (prob_grad - jnp.sum(prob_rows * prob_grad, axis=-1, keepdims=True)) * keep_rows
    ).astype(jnp.bfloat16)
    prob_kept = prob_bf * keep_rows.astype(jnp.bfloat16)
    grad_query = jnp.einsum(
        "bhqk,bkhe->bqhe", score_bf[..., :window_keys], key_win, preferred_element_type=jnp.float32
    )
    grad_query = (
        grad_query
        + jnp.einsum(
            "bhqk,khe->bqhe",
            score_bf[..., window_keys:],
            key_glob,
            preferred_element_type=jnp.float32,
        )
    ) * scaling
    flat_ids = block_ids.reshape(-1)
    window_blocks = (query_blocks, heads_here, BLOCK, 3 + RANDOM, BLOCK)
    key_part = (
        jnp.einsum(
            "bhqjk,bqhe->bjkhe",
            score_bf[..., :window_keys].reshape(window_blocks),
            query_blk,
            preferred_element_type=jnp.float32,
        )
        * scaling
    )
    key_globpart = (
        jnp.einsum(
            "bhqk,bqhe->khe",
            score_bf[..., window_keys:],
            query_blk,
            preferred_element_type=jnp.float32,
        )
        * scaling
    )
    value_part = jnp.einsum(
        "bhqjk,bqhe->bjkhe",
        prob_kept[..., :window_keys].reshape(window_blocks),
        delta_blk,
        preferred_element_type=jnp.float32,
    )
    value_globpart = jnp.einsum(
        "bhqk,bqhe->khe",
        prob_kept[..., window_keys:],
        delta_blk,
        preferred_element_type=jnp.float32,
    )
    block_hot = (block_ids[:, :, None] == jnp.arange(block_total, dtype=jnp.int32)).astype(
        jnp.float32
    )

    def place_blocks(parts):
        return jnp.einsum(
            "bjc,bjke->cke",
            block_hot,
            parts.reshape(query_blocks, 3 + RANDOM, BLOCK, columns),
            precision=lax.Precision.HIGH,
            preferred_element_type=jnp.float32,
        ).reshape(seq_length, columns)

    grad_key = place_blocks(key_part)
    grad_key = grad_key.at[doc_globals].add(key_globpart.reshape(global_count, columns))
    grad_value = place_blocks(value_part)
    grad_value = grad_value.at[doc_globals].add(value_globpart.reshape(global_count, columns))
    delta_glob = (
        jnp.einsum(
            "ng,nc->gc",
            picker,
            delta_head.reshape(query_count, columns),
            preferred_element_type=jnp.float32,
        )
        .astype(jnp.bfloat16)
        .reshape(global_count, heads_here, HEAD_DIM)
    )
    prob_grad_glob = jnp.einsum(
        "ghe,the->hgt", delta_glob, value_all, preferred_element_type=jnp.float32
    )
    score_glob_bf = (
        prob_glob * (prob_grad_glob - jnp.sum(prob_glob * prob_grad_glob, axis=-1, keepdims=True))
    ).astype(jnp.bfloat16)
    grad_query_glob = (
        jnp.einsum(
            "hgt,the->ghe", score_glob_bf, key_all, preferred_element_type=jnp.float32
        ).reshape(global_count, columns)
        * scaling
    )
    grad_key = (
        grad_key
        + jnp.einsum(
            "hgt,ghe->the", score_glob_bf, query_glob, preferred_element_type=jnp.float32
        ).reshape(seq_length, columns)
        * scaling
    )
    grad_value = grad_value + jnp.einsum(
        "hgt,ghe->the", prob_glob_bf, delta_glob, preferred_element_type=jnp.float32
    ).reshape(seq_length, columns)
    grad_query_all = grad_query.reshape(query_count, columns) + jnp.dot(
        picker_f, grad_query_glob, precision=lax.Precision.HIGHEST
    )
    def my_half(grads):
        halves = grads.reshape(seq_devices, splitting, slice_rows, columns)
        mine = jnp.where(my_slice == 0, halves[:, 0], halves[:, 1])
        theirs = jnp.where(my_slice == 0, halves[:, 1], halves[:, 0])
        received = lax.ppermute(theirs.astype(jnp.bfloat16), "sx", partner)
        return (mine + received.astype(jnp.float32)).astype(jnp.bfloat16)

    def to_positions(rows):
        back = lax.all_to_all(rows, SEQ_AXES, split_axis=0, concat_axis=0, tiled=True)
        return (
            back.reshape(head_groups, splitting, slice_rows, columns)
            .transpose(1, 2, 0, 3)
            .reshape(1, tokens, width)
        )

    grad_queries = to_positions(
        grad_query_all.astype(jnp.bfloat16).reshape(seq_devices, slice_rows, columns)
    )
    grad_keys = to_positions(my_half(grad_key))
    grad_values = to_positions(my_half(grad_value))
    return (grad_queries, grad_keys, grad_values, grad_out_proj)


def solution(mesh):
    seq_size, dp_size = mesh.shape["seq"], mesh.shape["dp"]
    torus = Mesh(
        mesh.devices.reshape(seq_size // 4, 4, dp_size // 2, 2), SEQ_AXES + DP_AXES
    )
    return jax.shard_map(
        shards,
        mesh=torus,
        in_specs=(
            P(DP_AXES, SEQ_AXES, None),
            P(DP_AXES, SEQ_AXES, None),
            P(DP_AXES, SEQ_AXES, None),
            P(DP_AXES, SEQ_AXES, None),
            P(DP_AXES, None, None),
            P(DP_AXES, None),
            P(DP_AXES, None),
        ),
        out_specs=(P(DP_AXES, SEQ_AXES, None), P(DP_AXES, SEQ_AXES, None), P(DP_AXES, SEQ_AXES, None), P(DP_AXES, None)),
        check_vma=False,
    )
```

```python
import math

import jax
import jax.numpy as jnp
from jax import lax
from jax.sharding import Mesh, PartitionSpec as P

HEAD_DIM = 128
BLOCK = 64
RANDOM = 3


MASKED = -1e30
SEQ_AXES = ("sz", "sx")
DP_AXES = ("dy", "dc")


def softmax_rows(scores):
    highest = jnp.max(scores, axis=-1, keepdims=True)
    raised = jnp.exp(scores - highest)
    return raised / jnp.sum(raised, axis=-1, keepdims=True)


def shards(query_rows, key_rows, value_rows, out_grad, rand_blocks, global_tokens, out_proj):
    seq_devices = lax.axis_size(SEQ_AXES)
    dp_devices = lax.axis_size(DP_AXES)
    tokens = query_rows.shape[1]
    width = query_rows.shape[2]
    model_width = out_grad.shape[2]
    head_count = width // HEAD_DIM
    splitting = max(seq_devices // head_count, 1)
    heads_here = max(head_count // seq_devices, 1)
    columns = heads_here * HEAD_DIM
    head_groups = seq_devices // splitting
    slice_rows = tokens // splitting
    seq_length = tokens * seq_devices
    block_total = seq_length // BLOCK
    window_keys = (3 + RANDOM) * BLOCK
    query_count = seq_devices * slice_rows
    query_blocks = query_count // BLOCK
    owned_groups = seq_devices // dp_devices // splitting
    global_count = global_tokens.shape[1]
    scaling = 1.0 / math.sqrt(HEAD_DIM)
    my_slice = lax.axis_index(SEQ_AXES) % splitting
    doc_blocks = rand_blocks[0]
    doc_globals = global_tokens[0]
    def head_rows(rows):
        return (
            rows[0]
            .reshape(splitting, slice_rows, head_groups, columns)
            .transpose(2, 0, 1, 3)
            .reshape(seq_devices, slice_rows, columns)
        )

    partner = [(i, i ^ 1) for i in range(lax.axis_size("sx"))]

    def both_halves(mine):
        other = lax.ppermute(mine, "sx", partner)
        low = jnp.where(my_slice == 0, mine, other)
        high = jnp.where(my_slice == 0, other, mine)
        return jnp.stack([low, high], axis=1).reshape(seq_devices, tokens, columns)

    def to_heads(rows):
        return lax.all_to_all(head_rows(rows), SEQ_AXES, split_axis=0, concat_axis=0, tiled=True)

    query_head = to_heads(query_rows)
    key_head = both_halves(to_heads(key_rows))
    value_head = both_halves(to_heads(value_rows))
    proj_rows = out_proj.reshape(owned_groups, columns, model_width)
    piece_rows = lax.all_gather(out_grad, DP_AXES, axis=0, tiled=True)
    doc_count = piece_rows.shape[0]
    grads = piece_rows.reshape(doc_count, splitting, slice_rows, model_width)
    local_delta = jnp.einsum(
        "kptd,gcd->kgptc", grads, proj_rows, preferred_element_type=jnp.float32
    ).astype(jnp.bfloat16)
    local_delta = local_delta.reshape(doc_count, owned_groups * splitting, slice_rows, columns)
    delta_blocks = local_delta
    delta_dp = lax.all_to_all(delta_blocks, DP_AXES, split_axis=0, concat_axis=1, tiled=True)
    delta_dp, query_head, key_head, value_head = lax.optimization_barrier(
        (delta_dp, query_head, key_head, value_head)
    )
    source_start = jnp.arange(seq_devices, dtype=jnp.int32)[:, None] * tokens
    offsets = jnp.arange(slice_rows, dtype=jnp.int32)[None, :]
    query_pos = (source_start + my_slice * slice_rows + offsets).reshape(query_count)
    block_of = query_pos.reshape(query_blocks, BLOCK)[:, 0] // BLOCK
    window = block_of[:, None] + jnp.arange(-1, 2, dtype=jnp.int32)[None, :]
    inside = (window >= 0) & (window < block_total)
    block_ids = jnp.concatenate(
        [jnp.clip(window, 0, block_total - 1), jnp.take(doc_blocks, block_of, axis=0)], axis=1
    )
    usable = jnp.concatenate(
        [jnp.repeat(inside, BLOCK, axis=1), jnp.ones((query_blocks, RANDOM * BLOCK), dtype=bool)],
        axis=1,
    )
    key_all = key_head.reshape(seq_length, heads_here, HEAD_DIM)
    value_all = value_head.reshape(seq_length, heads_here, HEAD_DIM)
    key_win = key_all.reshape(block_total, BLOCK, heads_here, HEAD_DIM)[block_ids].reshape(
        query_blocks, window_keys, heads_here, HEAD_DIM
    )
    value_win = value_all.reshape(block_total, BLOCK, heads_here, HEAD_DIM)[block_ids].reshape(
        query_blocks, window_keys, heads_here, HEAD_DIM
    )
    key_glob = jnp.take(key_all, doc_globals, axis=0)
    value_glob = jnp.take(value_all, doc_globals, axis=0)
    query_blk = query_head.reshape(query_blocks, BLOCK, heads_here, HEAD_DIM)
    score_win = (
        jnp.einsum("bqhe,bkhe->bhqk", query_blk, key_win, preferred_element_type=jnp.float32)
        * scaling
    )
    score_win = jnp.where(usable[:, None, None, :], score_win, MASKED)
    score_glob = (
        jnp.einsum("bqhe,khe->bhqk", query_blk, key_glob, preferred_element_type=jnp.float32)
        * scaling
    )
    prob_rows = softmax_rows(jnp.concatenate([score_win, score_glob], axis=-1))
    prob_bf = prob_rows.astype(jnp.bfloat16)
    sparse_out = jnp.einsum(
        "bhqk,bkhe->bqhe", prob_bf[..., :window_keys], value_win, preferred_element_type=jnp.float32
    )
    sparse_out = sparse_out + jnp.einsum(
        "bhqk,khe->bqhe", prob_bf[..., window_keys:], value_glob, preferred_element_type=jnp.float32
    )
    matches = query_pos[:, None] == doc_globals[None, :]
    picker = matches.astype(jnp.bfloat16)
    picker_f = matches.astype(jnp.float32)
    is_global = jnp.any(matches, axis=1)
    query_glob = (
        jnp.einsum(
            "ng,nc->gc",
            picker,
            query_head.reshape(query_count, columns),
            preferred_element_type=jnp.float32,
        )
        .astype(jnp.bfloat16)
        .reshape(global_count, heads_here, HEAD_DIM)
    )
    prob_glob = softmax_rows(
        jnp.einsum("ghe,the->hgt", query_glob, key_all, preferred_element_type=jnp.float32)
        * scaling
    )
    prob_glob_bf = prob_glob.astype(jnp.bfloat16)
    glob_out = jnp.einsum(
        "hgt,the->ghe", prob_glob_bf, value_all, preferred_element_type=jnp.float32
    ).reshape(global_count, columns)
    placed = jnp.dot(picker_f, glob_out, precision=lax.Precision.HIGHEST)
    attention = jnp.where(
        is_global[:, None], placed, sparse_out.reshape(query_count, columns)
    ).astype(jnp.bfloat16)
    owned = lax.all_to_all(
        lax.all_to_all(
            attention.reshape(1, seq_devices, slice_rows, columns),
            SEQ_AXES,
            split_axis=1,
            concat_axis=1,
            tiled=True,
        ),
        DP_AXES,
        split_axis=1,
        concat_axis=0,
        tiled=True,
    )
    owned = owned.reshape(dp_devices, owned_groups, splitting, slice_rows, columns)
    grad_sum = jnp.einsum("kgptc,kptd->gcd", owned, grads, preferred_element_type=jnp.float32)
    grad_sum, delta_blocks = (grad_sum, delta_blocks)
    z_size = lax.axis_size("sz")
    x_size = lax.axis_size("sx")
    proj_part = grad_sum.reshape(width // dp_devices, model_width).astype(jnp.bfloat16)
    z_rows = proj_part.shape[0] // (x_size * z_size)
    x_sum = jnp.sum(
        lax.all_to_all(
            proj_part.reshape(z_size, x_size, z_rows, model_width).transpose(1, 0, 2, 3),
            "sx",
            0,
            0,
            tiled=True,
        ).astype(jnp.float32),
        axis=0,
    )
    z_sum = jnp.sum(
        lax.all_to_all(
            x_sum.astype(jnp.bfloat16).reshape(z_size, z_rows, model_width), "sz", 0, 0, tiled=True
        ).astype(jnp.float32),
        axis=0,
    )
    grad_out_proj = lax.all_gather(z_sum.astype(jnp.bfloat16), SEQ_AXES, axis=0, tiled=True)
    delta_head = lax.all_to_all(
        delta_dp,
        SEQ_AXES,
        split_axis=1,
        concat_axis=1,
        tiled=True,
    )
    delta_blk = delta_head.reshape(query_blocks, BLOCK, heads_here, HEAD_DIM)
    prob_grad = jnp.concatenate(
        [
            jnp.einsum("bqhe,bkhe->bhqk", delta_blk, value_win, preferred_element_type=jnp.float32),
            jnp.einsum("bqhe,khe->bhqk", delta_blk, value_glob, preferred_element_type=jnp.float32),
        ],
        axis=-1,
    )
    keep_rows = (
        jnp.where(is_global, 0.0, 1.0).astype(jnp.float32).reshape(query_blocks, 1, BLOCK, 1)
    )
    score_bf = (
        prob_rows * (prob_grad - jnp.sum(prob_rows * prob_grad, axis=-1, keepdims=True)) * keep_rows
    ).astype(jnp.bfloat16)
    prob_kept = prob_bf * keep_rows.astype(jnp.bfloat16)
    grad_query = jnp.einsum(
        "bhqk,bkhe->bqhe", score_bf[..., :window_keys], key_win, preferred_element_type=jnp.float32
    )
    grad_query = (
        grad_query
        + jnp.einsum(
            "bhqk,khe->bqhe",
            score_bf[..., window_keys:],
            key_glob,
            preferred_element_type=jnp.float32,
        )
    ) * scaling
    flat_ids = block_ids.reshape(-1)
    window_blocks = (query_blocks, heads_here, BLOCK, 3 + RANDOM, BLOCK)
    key_part = (
        jnp.einsum(
            "bhqjk,bqhe->bjkhe",
            score_bf[..., :window_keys].reshape(window_blocks),
            query_blk,
            preferred_element_type=jnp.float32,
        )
        * scaling
    )
    key_globpart = (
        jnp.einsum(
            "bhqk,bqhe->khe",
            score_bf[..., window_keys:],
            query_blk,
            preferred_element_type=jnp.float32,
        )
        * scaling
    )
    value_part = jnp.einsum(
        "bhqjk,bqhe->bjkhe",
        prob_kept[..., :window_keys].reshape(window_blocks),
        delta_blk,
        preferred_element_type=jnp.float32,
    )
    value_globpart = jnp.einsum(
        "bhqk,bqhe->khe",
        prob_kept[..., window_keys:],
        delta_blk,
        preferred_element_type=jnp.float32,
    )
    block_hot = (block_ids[:, :, None] == jnp.arange(block_total, dtype=jnp.int32)).astype(
        jnp.float32
    )

    def place_blocks(parts):
        return jnp.einsum(
            "bjc,bjke->cke",
            block_hot,
            parts.reshape(query_blocks, 3 + RANDOM, BLOCK, columns),
            precision=lax.Precision.HIGH,
            preferred_element_type=jnp.float32,
        ).reshape(seq_length, columns)

    grad_key = place_blocks(key_part)
    grad_key = grad_key.at[doc_globals].add(key_globpart.reshape(global_count, columns))
    grad_value = place_blocks(value_part)
    grad_value = grad_value.at[doc_globals].add(value_globpart.reshape(global_count, columns))
    delta_glob = (
        jnp.einsum(
            "ng,nc->gc",
            picker,
            delta_head.reshape(query_count, columns),
            preferred_element_type=jnp.float32,
        )
        .astype(jnp.bfloat16)
        .reshape(global_count, heads_here, HEAD_DIM)
    )
    prob_grad_glob = jnp.einsum(
        "ghe,the->hgt", delta_glob, value_all, preferred_element_type=jnp.float32
    )
    score_glob_bf = (
        prob_glob * (prob_grad_glob - jnp.sum(prob_glob * prob_grad_glob, axis=-1, keepdims=True))
    ).astype(jnp.bfloat16)
    grad_query_glob = (
        jnp.einsum(
            "hgt,the->ghe", score_glob_bf, key_all, preferred_element_type=jnp.float32
        ).reshape(global_count, columns)
        * scaling
    )
    grad_key = (
        grad_key
        + jnp.einsum(
            "hgt,ghe->the", score_glob_bf, query_glob, preferred_element_type=jnp.float32
        ).reshape(seq_length, columns)
        * scaling
    )
    grad_value = grad_value + jnp.einsum(
        "hgt,ghe->the", prob_glob_bf, delta_glob, preferred_element_type=jnp.float32
    ).reshape(seq_length, columns)
    grad_query_all = grad_query.reshape(query_count, columns) + jnp.dot(
        picker_f, grad_query_glob, precision=lax.Precision.HIGHEST
    )
    def fold_pairs(grads):
        received = lax.all_to_all(
            grads.astype(jnp.bfloat16).reshape(seq_devices, tokens, columns),
            SEQ_AXES,
            split_axis=0,
            concat_axis=0,
            tiled=True,
        )
        summed = jnp.sum(
            received.astype(jnp.float32).reshape(head_groups, splitting, tokens, columns), axis=1
        )
        return summed.transpose(1, 0, 2).reshape(1, tokens, width).astype(jnp.bfloat16)

    def to_positions(rows):
        back = lax.all_to_all(rows, SEQ_AXES, split_axis=0, concat_axis=0, tiled=True)
        return (
            back.reshape(head_groups, splitting, slice_rows, columns)
            .transpose(1, 2, 0, 3)
            .reshape(1, tokens, width)
        )

    grad_queries = to_positions(
        grad_query_all.astype(jnp.bfloat16).reshape(seq_devices, slice_rows, columns)
    )
    grad_keys = fold_pairs(grad_key)
    grad_values = fold_pairs(grad_value)
    return (grad_queries, grad_keys, grad_values, grad_out_proj)


def solution(mesh):
    seq_size, dp_size = mesh.shape["seq"], mesh.shape["dp"]
    torus = Mesh(
        mesh.devices.reshape(seq_size // 4, 4, dp_size // 2, 2), SEQ_AXES + DP_AXES
    )
    return jax.shard_map(
        shards,
        mesh=torus,
        in_specs=(
            P(DP_AXES, SEQ_AXES, None),
            P(DP_AXES, SEQ_AXES, None),
            P(DP_AXES, SEQ_AXES, None),
            P(DP_AXES, SEQ_AXES, None),
            P(DP_AXES, None, None),
            P(DP_AXES, None),
            P(DP_AXES, None),
        ),
        out_specs=(P(DP_AXES, SEQ_AXES, None), P(DP_AXES, SEQ_AXES, None), P(DP_AXES, SEQ_AXES, None), P(DP_AXES, None)),
        check_vma=False,
    )
```
